32 devices in a mesh: visit: 8 (over z, x), sky: 4 (over y, core).
Axes of the slice: x: 2, y: 2, z: 4, core: 2. Of those that a mesh axis runs over, the one named last changes fastest.
Arguments:
- warped: bfloat16 [16, 512, 2048], P('visit', 'sky'), may hold values from -11 to 21
- inv_var: bfloat16 [16, 512, 2048], P('visit', 'sky'), may hold values from 0.19921875 to 5
- intersection: int32 [8, 4, 4], P('visit', 'sky'), may hold values from 0 to 3, as said below
- col_start: int32 [8, 4], P('visit', 'sky'), may hold values from 0 to 1536, as said below
- row_interp: bfloat16 [8, 4, 512, 512], P('visit', 'sky'), may hold values from -0.22 to 1.4, as said below
- col_interp: bfloat16 [8, 4, 512, 512], P('visit', 'sky'), may hold values from -0.22 to 1.4, as said below
- cell_ids: int32 [8, 4, 4, 4], P('visit', 'sky'), may hold values from 0 to 15
- kernels: bfloat16 [8, 4, 16, 121], P('visit', 'sky'), may hold values from -0.59765625 to 0.59765625
- science: bfloat16 [8, 4, 512, 512], P('visit', 'sky'), may hold values from -8 to 8
- inv_sigma: bfloat16 [8, 4, 512, 512], P('visit', 'sky'), may hold values from 0.29882812 to 1
Outputs:
- coadd: float32 [512, 2048], P('sky')
- outlier_weight: float32 [8, 4, 512, 512], P('visit', 'sky')
The draws below stay inside these ranges and needn't reach their ends.
Inputs may be any that keep to these rules, and one draw needn't show every extreme that they name: `intersection`: the 4 strip numbers of one tile are distinct. `col_start`: a multiple of 128. `row_interp`: nonzero only within two places of the diagonal, each row's diagonal entry larger than the sum of its other magnitudes. `col_interp`: nonzero only within two places of the diagonal, each row's diagonal entry larger than the sum of its other magnitudes.
All inputs are finite; a program needn't handle non-finite values.
Results may differ from the reference program's by a relative error of at most 0.0017.
Values may be sent and summed in bfloat16 or wider, within the bound.
No kernel may reach another device: no remote copies, remote signals or barrier semaphores. Data moves between devices by JAX's collectives and lax.ppermute only.
A program may use at most 64 MiB of HBM per device.

```python
import math
import jax
import jax.numpy as jnp
from jax import lax

GROUPS = 8
OWNERS = 4
VISITS = 16
STRIP = 128
NOV = 4
TILE = 512
SKY_W = 2048
SKY_ROWS = 512
KSIZE = 11
KTAPS = 121
CELL = 128
NCELL = 16
PASSES = 3


def draw_warped(key, part):
    shape_all = (VISITS, SKY_ROWS, SKY_W)
    sky_level = jnp.clip(jax.random.normal(jax.random.fold_in(key, 11), (SKY_ROWS, SKY_W), jnp.float32), -4.0, 4.0)
    noise_part = jnp.clip(jax.random.normal(jax.random.fold_in(key, 12), shape_all, jnp.float32), -4.0, 4.0)
    struck = jax.random.uniform(jax.random.fold_in(key, 13), shape_all, jnp.float32) < 0.03
    strength = jax.random.uniform(jax.random.fold_in(key, 14), shape_all, jnp.float32, 4.0, 10.0)
    return (sky_level[None] + noise_part + jnp.where(struck, strength, 0.0)).astype(jnp.bfloat16)


def draw_intersection(key, part):
    tile_keys = jax.random.split(jax.random.fold_in(key, 21), GROUPS * OWNERS)
    strip_orders = jax.vmap(lambda one_key: jax.random.permutation(one_key, OWNERS))(tile_keys)
    strip_orders = strip_orders.at[0].set(OWNERS - 1 - jnp.arange(OWNERS, dtype=jnp.int32))
    strip_orders = strip_orders.at[1].set(jnp.arange(OWNERS, dtype=jnp.int32))
    return strip_orders[:, :NOV].reshape(GROUPS, OWNERS, NOV).astype(jnp.int32)


def draw_col_start(key, part):
    steps_count = (SKY_W - TILE) // STRIP + 1
    starts = jax.random.randint(jax.random.fold_in(key, 31), (GROUPS, OWNERS), 0, steps_count) * STRIP
    starts = starts.at[0, 0].set(SKY_W - TILE)
    starts = starts.at[0, 1].set(0)
    return starts.astype(jnp.int32)


def band_matrix(key, spread, lowest):
    offsets = jnp.abs(jnp.arange(TILE)[None, :] - jnp.arange(TILE)[:, None])
    shape_all = (GROUPS, OWNERS, TILE, TILE)
    beside = jax.random.uniform(jax.random.fold_in(key, 41), shape_all, jnp.float32, -spread, spread)
    centre = jax.random.uniform(jax.random.fold_in(key, 42), shape_all, jnp.float32, lowest, lowest + 0.4)
    return jnp.where(offsets == 0, centre, jnp.where(offsets <= 2, beside, 0.0)).astype(jnp.bfloat16)


def draw_row_interp(key, part):
    return band_matrix(jax.random.fold_in(key, 51), 0.2, 0.9)


def draw_col_interp(key, part):
    return band_matrix(jax.random.fold_in(key, 52), 0.2, 0.9)


def touch_ends(drawn, key, low, high):
    shape = drawn.shape
    spot = [jax.random.randint(jax.random.fold_in(key, axis), (), 0, shape[axis]) for axis in range(len(shape))]
    drawn = drawn.at[tuple(spot)].set(low)
    longest = shape.index(max(shape))
    spot[longest] = (spot[longest] + 1) % shape[longest]
    return drawn.at[tuple(spot)].set(high)


def block_levels(own_key, shape, cuts, smallest, top_value):
    def one(position, blocks):
        steps = jax.random.uniform(jax.random.fold_in(jax.random.fold_in(own_key, 6), position), (blocks,), jnp.float32, smallest / len(cuts), top_value / len(cuts))
        return jnp.repeat(jnp.exp(steps), shape[position] // blocks).reshape((-1,) + (1,) * (len(shape) - position - 1))

    gain = one(*cuts[0])
    for cut in cuts[1:]:
        gain = gain * one(*cut)
    return gain


def scatter_about(rng, shape, scale, bound, cuts=(), kind=jnp.bfloat16):
    values = scale * jax.random.normal(rng, shape, jnp.float32)
    if cuts:
        values = values * block_levels(rng, shape, cuts, -0.22, 0.18)
    return jnp.clip(values, -bound, bound).astype(kind)


def setup_inputs(seed: int = 0) -> dict:
    splits = jax.random.split(jax.random.key(seed), 11)
    warped = draw_warped(jax.random.fold_in(splits[10], 71), 0)
    inv_var = jnp.clip(jnp.exp(math.log(5.0) - 3.2227897 * jax.random.uniform(splits[1], (VISITS, SKY_ROWS, SKY_W), jnp.float32) ** block_levels(splits[1], (VISITS, SKY_ROWS, SKY_W), ((0, 8), (1, 4)), -0.2, 0.2)), 0.19921875, 5.0).astype(jnp.bfloat16)
    intersection = draw_intersection(jax.random.fold_in(splits[10], 71), 0)
    col_start = draw_col_start(jax.random.fold_in(splits[10], 71), 0)
    row_interp = draw_row_interp(jax.random.fold_in(splits[10], 71), 0)
    col_interp = draw_col_interp(jax.random.fold_in(splits[10], 71), 0)
    cell_ids = touch_ends(jax.random.randint(splits[6], (GROUPS, OWNERS, TILE // CELL, TILE // CELL), 0, NCELL), jax.random.fold_in(splits[6], 1), 0, NCELL - 1).astype(jnp.int32)
    kernels = scatter_about(splits[7], (GROUPS, OWNERS, NCELL, KTAPS), 0.1, 0.59765625, ((0, 8), (1, 4)))
    science = scatter_about(splits[8], (GROUPS, OWNERS, TILE, TILE), 2.0, 8.0, ((0, 8), (1, 4)))
    inv_sigma = jnp.clip(jnp.exp(math.log(1.0) - 1.2078867 * jax.random.uniform(splits[9], (GROUPS, OWNERS, TILE, TILE), jnp.float32) ** block_levels(splits[9], (GROUPS, OWNERS, TILE, TILE), ((0, 8), (1, 4)), -0.2, 0.2)), 0.29882812, 1.0).astype(jnp.bfloat16)
    return dict(warped=warped, inv_var=inv_var, intersection=intersection, col_start=col_start, row_interp=row_interp, col_interp=col_interp, cell_ids=cell_ids, kernels=kernels, science=science, inv_sigma=inv_sigma)


CAUCHY = 2.0
OUTLIER = 3.0

def robust_coadd(warped, inv_var):
    values = warped.astype(jnp.float32)
    weights = inv_var.astype(jnp.float32)
    root_weight = jnp.sqrt(weights)
    coadd_field = lax.optimization_barrier(jnp.sum(weights * values, axis=0)) / lax.optimization_barrier(jnp.sum(weights, axis=0))
    for pass_index in range(PASSES):
        scaled = (values - coadd_field[None]) * root_weight / CAUCHY
        cauchy = weights / (1.0 + scaled * scaled)
        coadd_field = lax.optimization_barrier(jnp.sum(cauchy * values, axis=0)) / lax.optimization_barrier(jnp.sum(cauchy, axis=0))
    return coadd_field

def psf_match(blotted, cell_grid, kernel_table):
    half_width = KSIZE // 2
    padded = jnp.pad(blotted.astype(jnp.float32), half_width)
    taps_grid = kernel_table.astype(jnp.float32)[cell_grid]
    summed = jnp.zeros((TILE, TILE), jnp.float32)
    for offset_index in range(KSIZE * KSIZE):
        row_off = offset_index // KSIZE
        col_off = offset_index % KSIZE
        tap_field = jnp.repeat(jnp.repeat(taps_grid[:, :, offset_index], CELL, axis=0), CELL, axis=1)
        summed = summed + tap_field * padded[row_off:row_off + TILE, col_off:col_off + TILE]
    return summed

def reference(warped, inv_var, intersection, col_start, row_interp, col_interp, cell_ids, kernels, science, inv_sigma):
    coadd_field = robust_coadd(warped, inv_var)
    coadd_low = coadd_field.astype(jnp.bfloat16)
    tiles = GROUPS * OWNERS

    def one_tile(packed):
        strips, start_col, rows_map, cols_map, cell_grid, kernel_table, science_tile, sigma_tile = packed
        pieces = [lax.dynamic_slice(coadd_low, (strips[slot_number] * STRIP, start_col), (STRIP, TILE)) for slot_number in range(NOV)]
        footprint = jnp.concatenate(pieces, axis=0)
        projected = jnp.dot(rows_map, footprint, preferred_element_type=jnp.float32).astype(jnp.bfloat16)
        blotted = jnp.dot(projected, cols_map, preferred_element_type=jnp.float32).astype(jnp.bfloat16)
        matched = psf_match(blotted, cell_grid, kernel_table)
        residual = (science_tile.astype(jnp.float32) - matched) * sigma_tile.astype(jnp.float32) / OUTLIER
        return 1.0 / (1.0 + residual * residual)
    packed = (intersection.reshape(tiles, NOV), col_start.reshape(tiles), row_interp.reshape(tiles, TILE, TILE), col_interp.reshape(tiles, TILE, TILE), cell_ids.reshape(tiles, TILE // CELL, TILE // CELL), kernels.reshape(tiles, NCELL, KTAPS), science.reshape(tiles, TILE, TILE), inv_sigma.reshape(tiles, TILE, TILE))
    outlier = lax.map(one_tile, packed)
    return (coadd_field, outlier.reshape(GROUPS, OWNERS, TILE, TILE))
```

```python
import jax
import jax.numpy as jnp
from jax import lax
from jax.sharding import PartitionSpec as P

STRIP = 128
NOV = 4
TILE = 512
KSIZE = 11
CELL = 128
NCELL = 16
PASSES = 3


CAUCHY = 2.0
OUTLIER = 3.0


def local_coadd(values, weights):
    root_weight = jnp.sqrt(weights)
    coadd_field = jnp.sum(weights * values, axis=0) / jnp.sum(weights, axis=0)
    for pass_index in range(PASSES):
        scaled = (values - coadd_field[None]) * root_weight / CAUCHY
        cauchy = weights / (1.0 + scaled * scaled)
        coadd_field = jnp.sum(cauchy * values, axis=0) / jnp.sum(cauchy, axis=0)
    return coadd_field


def psf_match(blotted, cell_grid, kernel_table):
    tile_side = blotted.shape[1]
    blocks = tile_side // CELL
    half_width = KSIZE // 2
    window = CELL + KSIZE - 1
    picker = (cell_grid.reshape(-1)[:, None] == jnp.arange(NCELL, dtype=jnp.int32)[None, :]).astype(
        jnp.bfloat16
    )
    tap_rows = jnp.dot(picker, kernel_table, preferred_element_type=jnp.float32)
    tap_rows = tap_rows.reshape(blocks, blocks, KSIZE, KSIZE)
    source = jnp.arange(window, dtype=jnp.int32)[:, None]
    target = jnp.arange(CELL, dtype=jnp.int32)[None, :]
    diagonal = (
        (source - target)[None] == jnp.arange(KSIZE, dtype=jnp.int32)[:, None, None]
    ).astype(jnp.float32)
    banded_all = jnp.einsum(
        "xyab,bcl->xyacl", tap_rows, diagonal, precision=lax.Precision.HIGHEST
    ).astype(jnp.bfloat16)
    padded = jnp.pad(blotted, ((half_width, half_width), (half_width, half_width)))
    row_parts = []
    for row_block in range(blocks):
        rows_window = lax.slice_in_dim(padded, row_block * CELL, row_block * CELL + window, axis=0)
        col_parts = []
        for col_block in range(blocks):
            cols_window = lax.slice_in_dim(
                rows_window, col_block * CELL, col_block * CELL + window, axis=1
            )
            horizontal = jnp.einsum(
                "rc,acl->arl",
                cols_window,
                banded_all[row_block, col_block],
                preferred_element_type=jnp.float32,
            )
            summed = horizontal[0, 0:CELL, :]
            for tap_row in range(1, KSIZE):
                summed = summed + horizontal[tap_row, tap_row : tap_row + CELL, :]
            col_parts.append(summed)
        row_parts.append(jnp.concatenate(col_parts, axis=1))
    return jnp.concatenate(row_parts, axis=0)


def shards(
    warped,
    inv_var,
    intersection,
    col_start,
    row_interp,
    col_interp,
    cell_ids,
    kernels,
    science,
    inv_sigma,
):
    n_visit = lax.axis_size("visit")
    n_sky = lax.axis_size("sky")
    local_visits, strip_rows, sky_w = warped.shape
    stacked = jnp.stack([warped, inv_var], axis=0)
    chunk = strip_rows // n_visit
    stacked = stacked.reshape(2, local_visits, n_visit, chunk, sky_w)
    gathered = lax.all_to_all(stacked, "visit", split_axis=2, concat_axis=1, tiled=True)
    gathered = gathered.reshape(2, local_visits * n_visit, chunk, sky_w)
    row_share = local_coadd(gathered[0].astype(jnp.float32), gathered[1].astype(jnp.float32))
    coadd_field = lax.all_gather(row_share, "visit", axis=0, tiled=True)
    coadd_low = coadd_field.astype(jnp.bfloat16)

    start_col = col_start[0, 0]
    all_starts = lax.all_gather(col_start[0], "sky", axis=0, tiled=True)
    windows = jnp.stack(
        [lax.dynamic_slice_in_dim(coadd_low, all_starts[peer], TILE, 1) for peer in range(n_sky)],
        axis=0,
    )
    strips_here = lax.all_to_all(windows, "sky", split_axis=0, concat_axis=0, tiled=True)
    strips = intersection[0, 0]
    footprint = jnp.concatenate(
        [lax.dynamic_index_in_dim(strips_here, strips[slot], 0, keepdims=False) for slot in range(NOV)],
        axis=0,
    )
    projected = jnp.dot(row_interp[0, 0], footprint, preferred_element_type=jnp.float32).astype(
        jnp.bfloat16
    )
    blotted = jnp.dot(projected, col_interp[0, 0], preferred_element_type=jnp.float32).astype(
        jnp.bfloat16
    )
    matched = psf_match(blotted, cell_ids[0, 0], kernels[0, 0])
    residual = (
        (science[0, 0].astype(jnp.float32) - matched)
        * inv_sigma[0, 0].astype(jnp.float32)
        / OUTLIER
    )
    outlier = 1.0 / (1.0 + residual * residual)
    return (coadd_field, outlier[None, None])


def solution(mesh):
    in_specs = (
        P("visit", "sky", None),
        P("visit", "sky", None),
        P("visit", "sky", None),
        P("visit", "sky"),
        P("visit", "sky", None, None),
        P("visit", "sky", None, None),
        P("visit", "sky", None, None),
        P("visit", "sky", None, None),
        P("visit", "sky", None, None),
        P("visit", "sky", None, None),
    )
    out_specs = (P("sky", None), P("visit", "sky", None, None))
    return jax.shard_map(shards, mesh=mesh, in_specs=in_specs, out_specs=out_specs, check_vma=False)
```

```python
import jax
import jax.numpy as jnp
from jax import lax
from jax.sharding import PartitionSpec as P

STRIP = 128
NOV = 4
TILE = 512
KSIZE = 11
CELL = 128
NCELL = 16
PASSES = 3


CAUCHY = 2.0
OUTLIER = 3.0


def local_coadd(values, weights):
    root_weight = jnp.sqrt(weights)
    coadd_field = jnp.sum(weights * values, axis=0) / jnp.sum(weights, axis=0)
    for pass_index in range(PASSES):
        scaled = (values - coadd_field[None]) * root_weight / CAUCHY
        cauchy = weights / (1.0 + scaled * scaled)
        coadd_field = jnp.sum(cauchy * values, axis=0) / jnp.sum(cauchy, axis=0)
    return coadd_field


def psf_match(blotted, cell_grid, kernel_table):
    tile_side = blotted.shape[1]
    blocks = tile_side // CELL
    half_width = KSIZE // 2
    window = CELL + KSIZE - 1
    picker = (cell_grid.reshape(-1)[:, None] == jnp.arange(NCELL, dtype=jnp.int32)[None, :]).astype(
        jnp.bfloat16
    )
    tap_rows = jnp.dot(picker, kernel_table, preferred_element_type=jnp.float32)
    tap_rows = tap_rows.reshape(blocks, blocks, KSIZE, KSIZE)
    source = jnp.arange(window, dtype=jnp.int32)[:, None]
    target = jnp.arange(CELL, dtype=jnp.int32)[None, :]
    diagonal = (
        (source - target)[None] == jnp.arange(KSIZE, dtype=jnp.int32)[:, None, None]
    ).astype(jnp.float32)
    banded_all = jnp.einsum(
        "xyab,bcl->xyacl", tap_rows, diagonal, precision=lax.Precision.HIGHEST
    ).astype(jnp.bfloat16)
    padded = jnp.pad(blotted, ((half_width, half_width), (half_width, half_width)))
    row_parts = []
    for row_block in range(blocks):
        rows_window = lax.slice_in_dim(padded, row_block * CELL, row_block * CELL + window, axis=0)
        col_parts = []
        for col_block in range(blocks):
            cols_window = lax.slice_in_dim(
                rows_window, col_block * CELL, col_block * CELL + window, axis=1
            )
            horizontal = jnp.einsum(
                "rc,acl->arl",
                cols_window,
                banded_all[row_block, col_block],
                preferred_element_type=jnp.float32,
            )
            summed = horizontal[0, 0:CELL, :]
            for tap_row in range(1, KSIZE):
                summed = summed + horizontal[tap_row, tap_row : tap_row + CELL, :]
            col_parts.append(summed)
        row_parts.append(jnp.concatenate(col_parts, axis=1))
    return jnp.concatenate(row_parts, axis=0)


def shards(
    warped,
    inv_var,
    intersection,
    col_start,
    row_interp,
    col_interp,
    cell_ids,
    kernels,
    science,
    inv_sigma,
):
    n_visit = lax.axis_size("visit")
    n_sky = lax.axis_size("sky")
    local_visits, strip_rows, sky_w = warped.shape
    stacked = jnp.stack([warped, inv_var], axis=0)
    chunk = strip_rows // n_visit
    stacked = stacked.reshape(2, local_visits, n_visit, chunk, sky_w)
    gathered = lax.all_to_all(stacked, "visit", split_axis=2, concat_axis=1, tiled=True)
    gathered = gathered.reshape(2, local_visits * n_visit, chunk, sky_w)
    row_share = local_coadd(gathered[0].astype(jnp.float32), gathered[1].astype(jnp.float32))
    copies = jnp.broadcast_to(row_share[None], (n_visit,) + row_share.shape)
    coadd_field = lax.all_to_all(copies, "visit", split_axis=0, concat_axis=0, tiled=True)
    coadd_field = coadd_field.reshape(n_visit * chunk, sky_w)
    coadd_low = coadd_field.astype(jnp.bfloat16)

    start_col = col_start[0, 0]
    all_starts = lax.all_gather(col_start[0], "sky", axis=0, tiled=True)
    windows = jnp.stack(
        [lax.dynamic_slice_in_dim(coadd_low, all_starts[peer], TILE, 1) for peer in range(n_sky)],
        axis=0,
    )
    strips_here = lax.all_to_all(windows, "sky", split_axis=0, concat_axis=0, tiled=True)
    strips = intersection[0, 0]
    footprint = jnp.concatenate(
        [lax.dynamic_index_in_dim(strips_here, strips[slot], 0, keepdims=False) for slot in range(NOV)],
        axis=0,
    )
    projected = jnp.dot(row_interp[0, 0], footprint, preferred_element_type=jnp.float32).astype(
        jnp.bfloat16
    )
    blotted = jnp.dot(projected, col_interp[0, 0], preferred_element_type=jnp.float32).astype(
        jnp.bfloat16
    )
    matched = psf_match(blotted, cell_ids[0, 0], kernels[0, 0])
    residual = (
        (science[0, 0].astype(jnp.float32) - matched)
        * inv_sigma[0, 0].astype(jnp.float32)
        / OUTLIER
    )
    outlier = 1.0 / (1.0 + residual * residual)
    return (coadd_field, outlier[None, None])


def solution(mesh):
    in_specs = (
        P("visit", "sky", None),
        P("visit", "sky", None),
        P("visit", "sky", None),
        P("visit", "sky"),
        P("visit", "sky", None, None),
        P("visit", "sky", None, None),
        P("visit", "sky", None, None),
        P("visit", "sky", None, None),
        P("visit", "sky", None, None),
        P("visit", "sky", None, None),
    )
    out_specs = (P("sky", None), P("visit", "sky", None, None))
    return jax.shard_map(shards, mesh=mesh, in_specs=in_specs, out_specs=out_specs, check_vma=False)
```

```python
import jax
import jax.numpy as jnp
from jax import lax
from jax.sharding import PartitionSpec as P

STRIP = 128
NOV = 4
TILE = 512
KSIZE = 11
CELL = 128
NCELL = 16
PASSES = 3


CAUCHY = 2.0
OUTLIER = 3.0


def local_coadd(values, weights):
    root_weight = jnp.sqrt(weights)
    coadd_field = jnp.sum(weights * values, axis=0) / jnp.sum(weights, axis=0)
    for pass_index in range(PASSES):
        scaled = (values - coadd_field[None]) * root_weight / CAUCHY
        cauchy = weights / (1.0 + scaled * scaled)
        coadd_field = jnp.sum(cauchy * values, axis=0) / jnp.sum(cauchy, axis=0)
    return coadd_field


def psf_match(blotted, cell_grid, kernel_table):
    tile_side = blotted.shape[1]
    blocks = tile_side // CELL
    half_width = KSIZE // 2
    window = CELL + KSIZE - 1
    picker = (cell_grid.reshape(-1)[:, None] == jnp.arange(NCELL, dtype=jnp.int32)[None, :]).astype(
        jnp.bfloat16
    )
    tap_rows = jnp.dot(picker, kernel_table, preferred_element_type=jnp.float32)
    tap_rows = tap_rows.astype(jnp.bfloat16).reshape(blocks * blocks, KSIZE, KSIZE)
    source = jnp.arange(window, dtype=jnp.int32)[:, None]
    target = jnp.arange(CELL, dtype=jnp.int32)[None, :]
    diagonal = (
        (source - target)[None] == jnp.arange(KSIZE, dtype=jnp.int32)[:, None, None]
    ).astype(jnp.bfloat16)
    banded_all = jnp.einsum(
        "kab,bcl->kcal", tap_rows, diagonal, preferred_element_type=jnp.float32
    ).astype(jnp.bfloat16)
    banded_all = banded_all.reshape(blocks * blocks, window, KSIZE * CELL)
    padded = jnp.pad(blotted, ((half_width, half_width), (half_width, half_width)))
    row_parts = []
    for row_block in range(blocks):
        rows_window = lax.slice_in_dim(padded, row_block * CELL, row_block * CELL + window, axis=0)
        col_parts = []
        for col_block in range(blocks):
            cols_window = lax.slice_in_dim(
                rows_window, col_block * CELL, col_block * CELL + window, axis=1
            )
            horizontal = jnp.dot(
                cols_window,
                banded_all[row_block * blocks + col_block],
                preferred_element_type=jnp.float32,
            ).reshape(window, KSIZE, CELL)
            summed = horizontal[0:CELL, 0, :]
            for tap_row in range(1, KSIZE):
                summed = summed + horizontal[tap_row : tap_row + CELL, tap_row, :]
            col_parts.append(summed)
        row_parts.append(jnp.concatenate(col_parts, axis=1))
    return jnp.concatenate(row_parts, axis=0)


def shards(
    warped,
    inv_var,
    intersection,
    col_start,
    row_interp,
    col_interp,
    cell_ids,
    kernels,
    science,
    inv_sigma,
):
    n_visit = lax.axis_size("visit")
    n_sky = lax.axis_size("sky")
    local_visits, strip_rows, sky_w = warped.shape
    stacked = jnp.stack([warped, inv_var], axis=0)
    chunk = strip_rows // n_visit
    stacked = stacked.reshape(2, local_visits, n_visit, chunk, sky_w).transpose(2, 0, 1, 3, 4)
    stacked = stacked.reshape(n_visit, 2 * local_visits * chunk, sky_w)
    gathered = lax.all_to_all(stacked, "visit", split_axis=0, concat_axis=0, tiled=True)
    gathered = gathered.reshape(n_visit, 2, local_visits, chunk, sky_w)
    gathered = gathered.transpose(1, 0, 2, 3, 4).reshape(2, n_visit * local_visits, chunk, sky_w)
    row_share = local_coadd(gathered[0].astype(jnp.float32), gathered[1].astype(jnp.float32))
    copies = jnp.broadcast_to(row_share[None], (n_visit,) + row_share.shape)
    coadd_field = lax.all_to_all(copies, "visit", split_axis=0, concat_axis=0, tiled=True)
    coadd_field = coadd_field.reshape(n_visit * chunk, sky_w)
    coadd_low = coadd_field.astype(jnp.bfloat16)

    start_col = col_start[0, 0]
    all_starts = lax.all_gather(col_start[0], "sky", axis=0, tiled=True)
    windows = jnp.stack(
        [lax.dynamic_slice_in_dim(coadd_low, all_starts[peer], TILE, 1) for peer in range(n_sky)],
        axis=0,
    )
    strips_here = lax.all_to_all(windows, "sky", split_axis=0, concat_axis=0, tiled=True)
    strips = intersection[0, 0]
    footprint = jnp.concatenate(
        [lax.dynamic_index_in_dim(strips_here, strips[slot], 0, keepdims=False) for slot in range(NOV)],
        axis=0,
    )
    projected = jnp.dot(row_interp[0, 0], footprint, preferred_element_type=jnp.float32).astype(
        jnp.bfloat16
    )
    blotted = jnp.dot(projected, col_interp[0, 0], preferred_element_type=jnp.float32).astype(
        jnp.bfloat16
    )
    matched = psf_match(blotted, cell_ids[0, 0], kernels[0, 0])
    residual = (
        (science[0, 0].astype(jnp.float32) - matched)
        * inv_sigma[0, 0].astype(jnp.float32)
        / OUTLIER
    )
    outlier = 1.0 / (1.0 + residual * residual)
    return (coadd_field, outlier[None, None])


def solution(mesh):
    in_specs = (
        P("visit", "sky", None),
        P("visit", "sky", None),
        P("visit", "sky", None),
        P("visit", "sky"),
        P("visit", "sky", None, None),
        P("visit", "sky", None, None),
        P("visit", "sky", None, None),
        P("visit", "sky", None, None),
        P("visit", "sky", None, None),
        P("visit", "sky", None, None),
    )
    out_specs = (P("sky", None), P("visit", "sky", None, None))
    return jax.shard_map(shards, mesh=mesh, in_specs=in_specs, out_specs=out_specs, check_vma=False)
```

```python
import jax
import jax.numpy as jnp
from jax import lax
from jax.sharding import PartitionSpec as P

STRIP = 128
NOV = 4
TILE = 512
KSIZE = 11
CELL = 128
NCELL = 16
PASSES = 3


CAUCHY = 2.0
OUTLIER = 3.0


def local_coadd(values, weights):
    root_weight = jnp.sqrt(weights)
    coadd_field = jnp.sum(weights * values, axis=0) / jnp.sum(weights, axis=0)
    for pass_index in range(PASSES):
        scaled = (values - coadd_field[None]) * root_weight / CAUCHY
        cauchy = weights / (1.0 + scaled * scaled)
        coadd_field = jnp.sum(cauchy * values, axis=0) / jnp.sum(cauchy, axis=0)
    return coadd_field


def psf_match(blotted, cell_grid, kernel_table):
    tile_side = blotted.shape[1]
    blocks = tile_side // CELL
    half_width = KSIZE // 2
    window = CELL + KSIZE - 1
    picker = (cell_grid.reshape(-1)[:, None] == jnp.arange(NCELL, dtype=jnp.int32)[None, :]).astype(
        jnp.bfloat16
    )
    tap_rows = jnp.dot(picker, kernel_table, preferred_element_type=jnp.float32)
    tap_rows = tap_rows.astype(jnp.bfloat16).reshape(blocks * blocks, KSIZE, KSIZE)
    target = jnp.arange(CELL, dtype=jnp.int32)[:, None]
    source = jnp.arange(window, dtype=jnp.int32)[None, :]
    diagonal = (
        (source - target)[None] == jnp.arange(KSIZE, dtype=jnp.int32)[:, None, None]
    ).astype(jnp.bfloat16)
    vertical = jnp.einsum(
        "kab,ais->kbis", tap_rows, diagonal, preferred_element_type=jnp.float32
    ).astype(jnp.bfloat16)
    padded = jnp.pad(blotted, ((half_width, half_width), (half_width, half_width)))
    row_parts = []
    for row_block in range(blocks):
        rows_window = lax.slice_in_dim(padded, row_block * CELL, row_block * CELL + window, axis=0)
        col_parts = []
        for col_block in range(blocks):
            cols_window = lax.slice_in_dim(
                rows_window, col_block * CELL, col_block * CELL + window, axis=1
            )
            stacked = vertical[row_block * blocks + col_block].reshape(KSIZE * CELL, window)
            partial = jnp.dot(stacked, cols_window, preferred_element_type=jnp.float32)
            partial = partial.reshape(KSIZE, CELL, window)
            summed = partial[0, :, 0:CELL]
            for tap_col in range(1, KSIZE):
                summed = summed + partial[tap_col, :, tap_col : tap_col + CELL]
            col_parts.append(summed)
        row_parts.append(jnp.concatenate(col_parts, axis=1))
    return jnp.concatenate(row_parts, axis=0)


def shards(
    warped,
    inv_var,
    intersection,
    col_start,
    row_interp,
    col_interp,
    cell_ids,
    kernels,
    science,
    inv_sigma,
):
    n_visit = lax.axis_size("visit")
    n_sky = lax.axis_size("sky")
    local_visits, strip_rows, sky_w = warped.shape
    stacked = jnp.stack([warped, inv_var], axis=0)
    chunk = strip_rows // n_visit
    stacked = stacked.reshape(2, local_visits, n_visit, chunk, sky_w)
    gathered = lax.all_to_all(stacked, "visit", split_axis=2, concat_axis=1, tiled=True)
    gathered = gathered.reshape(2, local_visits * n_visit, chunk, sky_w)
    row_share = local_coadd(gathered[0].astype(jnp.float32), gathered[1].astype(jnp.float32))
    copies = jnp.broadcast_to(row_share[None], (n_visit,) + row_share.shape)
    coadd_field = lax.all_to_all(copies, "visit", split_axis=0, concat_axis=0, tiled=True)
    coadd_field = coadd_field.reshape(n_visit * chunk, sky_w)
    coadd_low = coadd_field.astype(jnp.bfloat16)

    start_col = col_start[0, 0]
    all_starts = lax.all_gather(col_start[0], "sky", axis=0, tiled=True)
    windows = jnp.stack(
        [lax.dynamic_slice_in_dim(coadd_low, all_starts[peer], TILE, 1) for peer in range(n_sky)],
        axis=0,
    )
    strips_here = lax.all_to_all(windows, "sky", split_axis=0, concat_axis=0, tiled=True)
    strips = intersection[0, 0]
    footprint = jnp.concatenate(
        [lax.dynamic_index_in_dim(strips_here, strips[slot], 0, keepdims=False) for slot in range(NOV)],
        axis=0,
    )
    projected = jnp.dot(row_interp[0, 0], footprint, preferred_element_type=jnp.float32).astype(
        jnp.bfloat16
    )
    blotted = jnp.dot(projected, col_interp[0, 0], preferred_element_type=jnp.float32).astype(
        jnp.bfloat16
    )
    matched = psf_match(blotted, cell_ids[0, 0], kernels[0, 0])
    residual = (
        (science[0, 0].astype(jnp.float32) - matched)
        * inv_sigma[0, 0].astype(jnp.float32)
        / OUTLIER
    )
    outlier = 1.0 / (1.0 + residual * residual)
    return (coadd_field, outlier[None, None])


def solution(mesh):
    in_specs = (
        P("visit", "sky", None),
        P("visit", "sky", None),
        P("visit", "sky", None),
        P("visit", "sky"),
        P("visit", "sky", None, None),
        P("visit", "sky", None, None),
        P("visit", "sky", None, None),
        P("visit", "sky", None, None),
        P("visit", "sky", None, None),
        P("visit", "sky", None, None),
    )
    out_specs = (P("sky", None), P("visit", "sky", None, None))
    return jax.shard_map(shards, mesh=mesh, in_specs=in_specs, out_specs=out_specs, check_vma=False)
```

```python
import jax
import jax.numpy as jnp
from jax import lax
from jax.sharding import PartitionSpec as P

STRIP = 128
NOV = 4
TILE = 512
KSIZE = 11
CELL = 128
NCELL = 16
PASSES = 3


CAUCHY = 2.0
OUTLIER = 3.0


def local_coadd(values, weights):
    root_weight = jnp.sqrt(weights)
    coadd_field = jnp.sum(weights * values, axis=0) / jnp.sum(weights, axis=0)
    for pass_index in range(PASSES):
        scaled = (values - coadd_field[None]) * root_weight / CAUCHY
        cauchy = weights / (1.0 + scaled * scaled)
        coadd_field = jnp.sum(cauchy * values, axis=0) / jnp.sum(cauchy, axis=0)
    return coadd_field


def psf_match(blotted, cell_grid, kernel_table):
    tile_side = blotted.shape[1]
    blocks = tile_side // CELL
    half_width = KSIZE // 2
    window = CELL + KSIZE - 1
    picker = (cell_grid.reshape(-1)[:, None] == jnp.arange(NCELL, dtype=jnp.int32)[None, :]).astype(
        jnp.bfloat16
    )
    tap_rows = jnp.dot(picker, kernel_table, preferred_element_type=jnp.float32)
    tap_rows = tap_rows.astype(jnp.bfloat16).reshape(blocks, blocks, KSIZE, KSIZE)
    source = jnp.arange(window, dtype=jnp.int32)[:, None]
    target = jnp.arange(CELL, dtype=jnp.int32)[None, :]
    diagonal = (
        (source - target)[None] == jnp.arange(KSIZE, dtype=jnp.int32)[:, None, None]
    ).astype(jnp.bfloat16)
    banded_all = jnp.einsum(
        "xyab,bcl->xyacl", tap_rows, diagonal, preferred_element_type=jnp.float32
    ).astype(jnp.bfloat16)
    padded = jnp.pad(blotted, ((half_width, half_width), (half_width, half_width)))
    row_parts = []
    for row_block in range(blocks):
        rows_window = lax.slice_in_dim(padded, row_block * CELL, row_block * CELL + window, axis=0)
        col_parts = []
        for col_block in range(blocks):
            cols_window = lax.slice_in_dim(
                rows_window, col_block * CELL, col_block * CELL + window, axis=1
            )
            horizontal = jnp.einsum(
                "rc,acl->arl",
                cols_window,
                banded_all[row_block, col_block],
                preferred_element_type=jnp.float32,
            )
            summed = horizontal[0, 0:CELL, :]
            for tap_row in range(1, KSIZE):
                summed = summed + horizontal[tap_row, tap_row : tap_row + CELL, :]
            col_parts.append(summed)
        row_parts.append(jnp.concatenate(col_parts, axis=1))
    return jnp.concatenate(row_parts, axis=0)


def shards(
    warped,
    inv_var,
    intersection,
    col_start,
    row_interp,
    col_interp,
    cell_ids,
    kernels,
    science,
    inv_sigma,
):
    n_visit = lax.axis_size("visit")
    n_sky = lax.axis_size("sky")
    local_visits, strip_rows, sky_w = warped.shape
    stacked = jnp.stack([warped, inv_var], axis=0)
    chunk = strip_rows // n_visit
    stacked = stacked.reshape(2, local_visits, n_visit, chunk, sky_w)
    gathered = lax.all_to_all(stacked, "visit", split_axis=2, concat_axis=1, tiled=True)
    gathered = gathered.reshape(2, local_visits * n_visit, chunk, sky_w)
    row_share = local_coadd(gathered[0].astype(jnp.float32), gathered[1].astype(jnp.float32))
    copies = jnp.broadcast_to(row_share[None], (n_visit,) + row_share.shape)
    coadd_field = lax.all_to_all(copies, "visit", split_axis=0, concat_axis=0, tiled=True)
    coadd_field = coadd_field.reshape(n_visit * chunk, sky_w)
    coadd_low = coadd_field.astype(jnp.bfloat16)

    start_col = col_start[0, 0]
    all_starts = lax.all_gather(col_start[0], "sky", axis=0, tiled=True)
    windows = jnp.stack(
        [lax.dynamic_slice_in_dim(coadd_low, all_starts[peer], TILE, 1) for peer in range(n_sky)],
        axis=0,
    )
    strips_here = lax.all_to_all(windows, "sky", split_axis=0, concat_axis=0, tiled=True)
    strips = intersection[0, 0]
    footprint = jnp.concatenate(
        [lax.dynamic_index_in_dim(strips_here, strips[slot], 0, keepdims=False) for slot in range(NOV)],
        axis=0,
    )
    projected = jnp.dot(row_interp[0, 0], footprint, preferred_element_type=jnp.float32).astype(
        jnp.bfloat16
    )
    blotted = jnp.dot(projected, col_interp[0, 0], preferred_element_type=jnp.float32).astype(
        jnp.bfloat16
    )
    matched = psf_match(blotted, cell_ids[0, 0], kernels[0, 0])
    residual = (
        (science[0, 0].astype(jnp.float32) - matched)
        * inv_sigma[0, 0].astype(jnp.float32)
        / OUTLIER
    )
    outlier = 1.0 / (1.0 + residual * residual)
    return (coadd_field, outlier[None, None])


def solution(mesh):
    in_specs = (
        P("visit", "sky", None),
        P("visit", "sky", None),
        P("visit", "sky", None),
        P("visit", "sky"),
        P("visit", "sky", None, None),
        P("visit", "sky", None, None),
        P("visit", "sky", None, None),
        P("visit", "sky", None, None),
        P("visit", "sky", None, None),
        P("visit", "sky", None, None),
    )
    out_specs = (P("sky", None), P("visit", "sky", None, None))
    return jax.shard_map(shards, mesh=mesh, in_specs=in_specs, out_specs=out_specs, check_vma=False)
```

```python
import jax
import jax.numpy as jnp
from jax import lax
from jax.sharding import PartitionSpec as P

STRIP = 128
NOV = 4
TILE = 512
KSIZE = 11
CELL = 128
NCELL = 16
PASSES = 3


CAUCHY = 2.0
OUTLIER = 3.0


def local_coadd(values, weights):
    root_weight = jnp.sqrt(weights)
    coadd_field = jnp.sum(weights * values, axis=0) / jnp.sum(weights, axis=0)
    for pass_index in range(PASSES):
        scaled = (values - coadd_field[None]) * root_weight / CAUCHY
        cauchy = weights / (1.0 + scaled * scaled)
        coadd_field = jnp.sum(cauchy * values, axis=0) / jnp.sum(cauchy, axis=0)
    return coadd_field


def psf_match(blotted, cell_grid, kernel_table):
    tile_side = blotted.shape[1]
    blocks = tile_side // CELL
    half_width = KSIZE // 2
    window = CELL + KSIZE - 1
    picker = (cell_grid.reshape(-1)[:, None] == jnp.arange(NCELL, dtype=jnp.int32)[None, :]).astype(
        jnp.bfloat16
    )
    tap_rows = jnp.dot(picker, kernel_table, preferred_element_type=jnp.float32)
    tap_rows = tap_rows.astype(jnp.bfloat16).reshape(blocks, blocks, KSIZE, KSIZE)
    source = jnp.arange(window, dtype=jnp.int32)[:, None]
    target = jnp.arange(CELL, dtype=jnp.int32)[None, :]
    diagonal = (
        (source - target)[None] == jnp.arange(KSIZE, dtype=jnp.int32)[:, None, None]
    ).astype(jnp.bfloat16)
    banded_all = jnp.einsum(
        "xyab,bcl->xyacl", tap_rows, diagonal, preferred_element_type=jnp.float32
    ).astype(jnp.bfloat16)
    padded = jnp.pad(blotted, ((half_width, half_width), (half_width, half_width)))
    row_parts = []
    for row_block in range(blocks):
        rows_window = lax.slice_in_dim(padded, row_block * CELL, row_block * CELL + window, axis=0)
        col_parts = []
        for col_block in range(blocks):
            cols_window = lax.slice_in_dim(
                rows_window, col_block * CELL, col_block * CELL + window, axis=1
            )
            horizontal = jnp.einsum(
                "rc,acl->arl",
                cols_window,
                banded_all[row_block, col_block],
                preferred_element_type=jnp.float32,
            )
            summed = horizontal[0, 0:CELL, :]
            for tap_row in range(1, KSIZE):
                summed = summed + horizontal[tap_row, tap_row : tap_row + CELL, :]
            col_parts.append(summed)
        row_parts.append(jnp.concatenate(col_parts, axis=1))
    return jnp.concatenate(row_parts, axis=0)


def shards(
    warped,
    inv_var,
    intersection,
    col_start,
    row_interp,
    col_interp,
    cell_ids,
    kernels,
    science,
    inv_sigma,
):
    n_visit = lax.axis_size("visit")
    n_sky = lax.axis_size("sky")
    local_visits, strip_rows, sky_w = warped.shape
    stacked = jnp.stack([warped, inv_var], axis=0)
    all_starts = lax.all_gather(col_start[0], "sky", axis=0, tiled=True)
    peer_starts = tuple(all_starts[peer] for peer in range(n_sky))
    strip_ids = tuple(intersection[0, 0, slot] for slot in range(NOV))
    stacked, peer_starts, strip_ids = lax.optimization_barrier((stacked, peer_starts, strip_ids))
    chunk = strip_rows // n_visit
    stacked = stacked.reshape(2, local_visits, n_visit, chunk, sky_w)
    gathered = lax.all_to_all(stacked, "visit", split_axis=2, concat_axis=1, tiled=True)
    gathered = gathered.reshape(2, local_visits * n_visit, chunk, sky_w)
    row_share = local_coadd(gathered[0].astype(jnp.float32), gathered[1].astype(jnp.float32))
    copies = jnp.broadcast_to(row_share[None], (n_visit,) + row_share.shape)
    coadd_field = lax.all_to_all(copies, "visit", split_axis=0, concat_axis=0, tiled=True)
    coadd_field = coadd_field.reshape(n_visit * chunk, sky_w)
    coadd_low = coadd_field.astype(jnp.bfloat16)

    windows = jnp.stack(
        [lax.dynamic_slice_in_dim(coadd_low, peer_starts[peer], TILE, 1) for peer in range(n_sky)],
        axis=0,
    )
    strips_here = lax.all_to_all(windows, "sky", split_axis=0, concat_axis=0, tiled=True)
    footprint = jnp.concatenate(
        [lax.dynamic_index_in_dim(strips_here, strip_ids[slot], 0, keepdims=False) for slot in range(NOV)],
        axis=0,
    )
    projected = jnp.dot(row_interp[0, 0], footprint, preferred_element_type=jnp.float32).astype(
        jnp.bfloat16
    )
    blotted = jnp.dot(projected, col_interp[0, 0], preferred_element_type=jnp.float32).astype(
        jnp.bfloat16
    )
    matched = psf_match(blotted, cell_ids[0, 0], kernels[0, 0])
    residual = (
        (science[0, 0].astype(jnp.float32) - matched)
        * inv_sigma[0, 0].astype(jnp.float32)
        / OUTLIER
    )
    outlier = 1.0 / (1.0 + residual * residual)
    return (coadd_field, outlier[None, None])


def solution(mesh):
    in_specs = (
        P("visit", "sky", None),
        P("visit", "sky", None),
        P("visit", "sky", None),
        P("visit", "sky"),
        P("visit", "sky", None, None),
        P("visit", "sky", None, None),
        P("visit", "sky", None, None),
        P("visit", "sky", None, None),
        P("visit", "sky", None, None),
        P("visit", "sky", None, None),
    )
    out_specs = (P("sky", None), P("visit", "sky", None, None))
    return jax.shard_map(shards, mesh=mesh, in_specs=in_specs, out_specs=out_specs, check_vma=False)
```

```python
import jax
import jax.numpy as jnp
from jax import lax
from jax.sharding import PartitionSpec as P


NOV = 4
TILE = 512
KSIZE = 11
CELL = 128
NCELL = 16
PASSES = 3


CAUCHY = 2.0
OUTLIER = 3.0


def local_coadd(values, weights):
    root_weight = jnp.sqrt(weights)
    coadd_field = jnp.sum(weights * values, axis=0) / jnp.sum(weights, axis=0)
    for _ in range(PASSES):
        scaled = (values - coadd_field[None]) * root_weight / CAUCHY
        cauchy = weights / (1.0 + scaled * scaled)
        coadd_field = jnp.sum(cauchy * values, axis=0) / jnp.sum(cauchy, axis=0)
    return coadd_field


def psf_bands(cell_grid, kernel_table):
    blocks = TILE // CELL
    window = CELL + KSIZE - 1
    picker = (cell_grid.reshape(-1)[:, None] == jnp.arange(NCELL, dtype=jnp.int32)[None, :]).astype(
        jnp.bfloat16
    )
    tap_rows = jnp.dot(picker, kernel_table, preferred_element_type=jnp.float32)
    tap_rows = tap_rows.astype(jnp.bfloat16).reshape(blocks, blocks, KSIZE, KSIZE)
    source = jnp.arange(window, dtype=jnp.int32)[:, None]
    target = jnp.arange(CELL, dtype=jnp.int32)[None, :]
    diagonal = (
        (source - target)[None] == jnp.arange(KSIZE, dtype=jnp.int32)[:, None, None]
    ).astype(jnp.bfloat16)
    banded_all = jnp.einsum(
        "xyab,bcl->xyacl", tap_rows, diagonal, preferred_element_type=jnp.float32
    ).astype(jnp.bfloat16)
    return tuple(banded_all[r, c] for r in range(blocks) for c in range(blocks))


def psf_match(blotted, bands):
    tile_side = blotted.shape[1]
    blocks = tile_side // CELL
    half_width = KSIZE // 2
    window = CELL + KSIZE - 1
    padded = jnp.pad(blotted, ((half_width, half_width), (half_width, half_width)))
    row_parts = []
    for row_block in range(blocks):
        rows_window = lax.slice_in_dim(padded, row_block * CELL, row_block * CELL + window, axis=0)
        col_parts = []
        for col_block in range(blocks):
            cols_window = lax.slice_in_dim(
                rows_window, col_block * CELL, col_block * CELL + window, axis=1
            )
            horizontal = jnp.einsum(
                "rc,acl->arl",
                cols_window,
                bands[row_block * blocks + col_block],
                preferred_element_type=jnp.float32,
            )
            summed = horizontal[0, 0:CELL, :]
            for tap_row in range(1, KSIZE):
                summed = summed + horizontal[tap_row, tap_row : tap_row + CELL, :]
            col_parts.append(summed)
        row_parts.append(jnp.concatenate(col_parts, axis=1))
    return jnp.concatenate(row_parts, axis=0)


def shards(
    warped,
    inv_var,
    intersection,
    col_start,
    row_interp,
    col_interp,
    cell_ids,
    kernels,
    science,
    inv_sigma,
):
    n_visit = lax.axis_size("visit")
    n_sky = lax.axis_size("sky")
    _, strip_rows, sky_w = warped.shape
    chunk = strip_rows // n_visit
    values_all = lax.all_to_all(warped, "visit", split_axis=1, concat_axis=0, tiled=True)
    bands = psf_bands(cell_ids[0, 0], kernels[0, 0])
    weights_all = lax.all_to_all(inv_var, "visit", split_axis=1, concat_axis=0, tiled=True)
    values_all, bands = lax.optimization_barrier((values_all, bands))
    row_share = local_coadd(values_all.astype(jnp.float32), weights_all.astype(jnp.float32))
    copies = jnp.broadcast_to(row_share[None], (n_visit,) + row_share.shape)
    coadd_field = lax.all_to_all(copies, "visit", split_axis=0, concat_axis=0, tiled=True)
    coadd_field = coadd_field.reshape(n_visit * chunk, sky_w)
    coadd_low = coadd_field.astype(jnp.bfloat16)

    all_starts = lax.all_gather(col_start[0], "sky", axis=0, tiled=True)
    windows = jnp.stack(
        [lax.dynamic_slice_in_dim(coadd_low, all_starts[peer], TILE, 1) for peer in range(n_sky)],
        axis=0,
    )
    strips_here = lax.all_to_all(windows, "sky", split_axis=0, concat_axis=0, tiled=True)
    strips = intersection[0, 0]
    footprint = jnp.concatenate(
        [lax.dynamic_index_in_dim(strips_here, strips[slot], 0, keepdims=False) for slot in range(NOV)],
        axis=0,
    )
    projected = jnp.dot(row_interp[0, 0], footprint, preferred_element_type=jnp.float32).astype(
        jnp.bfloat16
    )
    blotted = jnp.dot(projected, col_interp[0, 0], preferred_element_type=jnp.float32).astype(
        jnp.bfloat16
    )
    matched = psf_match(blotted, bands)
    residual = (
        (science[0, 0].astype(jnp.float32) - matched)
        * inv_sigma[0, 0].astype(jnp.float32)
        / OUTLIER
    )
    outlier = 1.0 / (1.0 + residual * residual)
    return (coadd_field, outlier[None, None])


def solution(mesh):
    in_specs = (
        P("visit", "sky", None),
        P("visit", "sky", None),
        P("visit", "sky", None),
        P("visit", "sky"),
        P("visit", "sky", None, None),
        P("visit", "sky", None, None),
        P("visit", "sky", None, None),
        P("visit", "sky", None, None),
        P("visit", "sky", None, None),
        P("visit", "sky", None, None),
    )
    out_specs = (P("sky", None), P("visit", "sky", None, None))
    return jax.shard_map(shards, mesh=mesh, in_specs=in_specs, out_specs=out_specs, check_vma=False)
```

```python
import jax
import jax.numpy as jnp
from jax import lax
from jax.sharding import PartitionSpec as P


NOV = 4
TILE = 512
KSIZE = 11
CELL = 128
NCELL = 16
PASSES = 3


CAUCHY = 2.0
OUTLIER = 3.0


def local_coadd(values, weights):
    root_weight = jnp.sqrt(weights)
    coadd_field = jnp.sum(weights * values, axis=0) / jnp.sum(weights, axis=0)
    for _ in range(PASSES):
        scaled = (values - coadd_field[None]) * root_weight / CAUCHY
        cauchy = weights / (1.0 + scaled * scaled)
        coadd_field = jnp.sum(cauchy * values, axis=0) / jnp.sum(cauchy, axis=0)
    return coadd_field


def psf_taps(cell_grid, kernel_table):
    blocks = TILE // CELL
    picker = (cell_grid.reshape(-1)[:, None] == jnp.arange(NCELL, dtype=jnp.int32)[None, :]).astype(
        jnp.bfloat16
    )
    tap_rows = jnp.dot(picker, kernel_table, preferred_element_type=jnp.float32)
    return tap_rows.astype(jnp.bfloat16).reshape(blocks, blocks, KSIZE, KSIZE)


def psf_bands(tap_rows):
    blocks = TILE // CELL
    window = CELL + KSIZE - 1
    source = jnp.arange(window, dtype=jnp.int32)[:, None]
    target = jnp.arange(CELL, dtype=jnp.int32)[None, :]
    diagonal = (
        (source - target)[None] == jnp.arange(KSIZE, dtype=jnp.int32)[:, None, None]
    ).astype(jnp.bfloat16)
    banded_all = jnp.einsum(
        "xyab,bcl->xyacl", tap_rows, diagonal, preferred_element_type=jnp.float32
    ).astype(jnp.bfloat16)
    return tuple(banded_all[r, c] for r in range(blocks) for c in range(blocks))


def psf_match(blotted, bands):
    tile_side = blotted.shape[1]
    blocks = tile_side // CELL
    half_width = KSIZE // 2
    window = CELL + KSIZE - 1
    padded = jnp.pad(blotted, ((half_width, half_width), (half_width, half_width)))
    row_parts = []
    for row_block in range(blocks):
        rows_window = lax.slice_in_dim(padded, row_block * CELL, row_block * CELL + window, axis=0)
        col_parts = []
        for col_block in range(blocks):
            cols_window = lax.slice_in_dim(
                rows_window, col_block * CELL, col_block * CELL + window, axis=1
            )
            horizontal = jnp.einsum(
                "rc,acl->arl",
                cols_window,
                bands[row_block * blocks + col_block],
                preferred_element_type=jnp.float32,
            )
            summed = horizontal[0, 0:CELL, :]
            for tap_row in range(1, KSIZE):
                summed = summed + horizontal[tap_row, tap_row : tap_row + CELL, :]
            col_parts.append(summed)
        row_parts.append(jnp.concatenate(col_parts, axis=1))
    return jnp.concatenate(row_parts, axis=0)


def shards(
    warped,
    inv_var,
    intersection,
    col_start,
    row_interp,
    col_interp,
    cell_ids,
    kernels,
    science,
    inv_sigma,
):
    n_visit = lax.axis_size("visit")
    n_sky = lax.axis_size("sky")
    local_visits, strip_rows, sky_w = warped.shape
    stacked = jnp.stack([warped, inv_var], axis=0)
    tap_rows = psf_taps(cell_ids[0, 0], kernels[0, 0])
    stacked, tap_rows = lax.optimization_barrier((stacked, tap_rows))
    chunk = strip_rows // n_visit
    stacked = stacked.reshape(2, local_visits, n_visit, chunk, sky_w)
    gathered = lax.all_to_all(stacked, "visit", split_axis=2, concat_axis=1, tiled=True)
    gathered = gathered.reshape(2, local_visits * n_visit, chunk, sky_w)
    row_share = local_coadd(gathered[0].astype(jnp.float32), gathered[1].astype(jnp.float32))
    copies = jnp.broadcast_to(row_share[None], (n_visit,) + row_share.shape)
    coadd_field = lax.all_to_all(copies, "visit", split_axis=0, concat_axis=0, tiled=True)
    bands = psf_bands(tap_rows)
    coadd_field = coadd_field.reshape(n_visit * chunk, sky_w)
    coadd_low = coadd_field.astype(jnp.bfloat16)

    all_starts = lax.all_gather(col_start[0], "sky", axis=0, tiled=True)
    windows = jnp.stack(
        [lax.dynamic_slice_in_dim(coadd_low, all_starts[peer], TILE, 1) for peer in range(n_sky)],
        axis=0,
    )
    strips_here = lax.all_to_all(windows, "sky", split_axis=0, concat_axis=0, tiled=True)
    strips = intersection[0, 0]
    footprint = jnp.concatenate(
        [lax.dynamic_index_in_dim(strips_here, strips[slot], 0, keepdims=False) for slot in range(NOV)],
        axis=0,
    )
    projected = jnp.dot(row_interp[0, 0], footprint, preferred_element_type=jnp.float32).astype(
        jnp.bfloat16
    )
    blotted = jnp.dot(projected, col_interp[0, 0], preferred_element_type=jnp.float32).astype(
        jnp.bfloat16
    )
    matched = psf_match(blotted, bands)
    residual = (
        (science[0, 0].astype(jnp.float32) - matched)
        * inv_sigma[0, 0].astype(jnp.float32)
        / OUTLIER
    )
    outlier = 1.0 / (1.0 + residual * residual)
    return (coadd_field, outlier[None, None])


def solution(mesh):
    in_specs = (
        P("visit", "sky", None),
        P("visit", "sky", None),
        P("visit", "sky", None),
        P("visit", "sky"),
        P("visit", "sky", None, None),
        P("visit", "sky", None, None),
        P("visit", "sky", None, None),
        P("visit", "sky", None, None),
        P("visit", "sky", None, None),
        P("visit", "sky", None, None),
    )
    out_specs = (P("sky", None), P("visit", "sky", None, None))
    return jax.shard_map(shards, mesh=mesh, in_specs=in_specs, out_specs=out_specs, check_vma=False)
```

```python
import jax
import jax.numpy as jnp
from jax import lax
from jax.sharding import PartitionSpec as P


NOV = 4
TILE = 512
KSIZE = 11
CELL = 128
NCELL = 16
PASSES = 3


CAUCHY = 2.0
OUTLIER = 3.0


def local_coadd(values, weights):
    root_weight = jnp.sqrt(weights)
    coadd_field = jnp.sum(weights * values, axis=0) / jnp.sum(weights, axis=0)
    for _ in range(PASSES):
        scaled = (values - coadd_field[None]) * root_weight / CAUCHY
        cauchy = weights / (1.0 + scaled * scaled)
        coadd_field = jnp.sum(cauchy * values, axis=0) / jnp.sum(cauchy, axis=0)
    return coadd_field


def psf_taps(cell_grid, kernel_table):
    blocks = TILE // CELL
    picker = (cell_grid.reshape(-1)[:, None] == jnp.arange(NCELL, dtype=jnp.int32)[None, :]).astype(
        jnp.bfloat16
    )
    tap_rows = jnp.dot(picker, kernel_table, preferred_element_type=jnp.float32)
    return tap_rows.astype(jnp.bfloat16).reshape(blocks, blocks, KSIZE, KSIZE)


def psf_bands(tap_rows):
    blocks = TILE // CELL
    window = CELL + KSIZE - 1
    source = jnp.arange(window, dtype=jnp.int32)[:, None]
    target = jnp.arange(CELL, dtype=jnp.int32)[None, :]
    diagonal = (
        (source - target)[None] == jnp.arange(KSIZE, dtype=jnp.int32)[:, None, None]
    ).astype(jnp.bfloat16)
    banded_all = jnp.einsum(
        "xyab,bcl->xyacl", tap_rows, diagonal, preferred_element_type=jnp.float32
    ).astype(jnp.bfloat16)
    return tuple(banded_all[r, c] for r in range(blocks) for c in range(blocks))


def psf_match(blotted, bands):
    tile_side = blotted.shape[1]
    blocks = tile_side // CELL
    half_width = KSIZE // 2
    window = CELL + KSIZE - 1
    padded = jnp.pad(blotted, ((half_width, half_width), (half_width, half_width)))
    row_parts = []
    for row_block in range(blocks):
        rows_window = lax.slice_in_dim(padded, row_block * CELL, row_block * CELL + window, axis=0)
        col_parts = []
        for col_block in range(blocks):
            cols_window = lax.slice_in_dim(
                rows_window, col_block * CELL, col_block * CELL + window, axis=1
            )
            horizontal = jnp.einsum(
                "rc,acl->arl",
                cols_window,
                bands[row_block * blocks + col_block],
                preferred_element_type=jnp.float32,
            )
            summed = horizontal[0, 0:CELL, :]
            for tap_row in range(1, KSIZE):
                summed = summed + horizontal[tap_row, tap_row : tap_row + CELL, :]
            col_parts.append(summed)
        row_parts.append(jnp.concatenate(col_parts, axis=1))
    return jnp.concatenate(row_parts, axis=0)


def shards(
    warped,
    inv_var,
    intersection,
    col_start,
    row_interp,
    col_interp,
    cell_ids,
    kernels,
    science,
    inv_sigma,
):
    n_visit = lax.axis_size("visit")
    n_sky = lax.axis_size("sky")
    local_visits, strip_rows, sky_w = warped.shape
    stacked = jnp.stack([warped, inv_var], axis=0)
    tap_rows = psf_taps(cell_ids[0, 0], kernels[0, 0])
    strip_ids = tuple(intersection[0, 0, slot] for slot in range(NOV))
    stacked, tap_rows, strip_ids = lax.optimization_barrier((stacked, tap_rows, strip_ids))
    chunk = strip_rows // n_visit
    stacked = stacked.reshape(2, local_visits, n_visit, chunk, sky_w)
    gathered = lax.all_to_all(stacked, "visit", split_axis=2, concat_axis=1, tiled=True)
    gathered = gathered.reshape(2, local_visits * n_visit, chunk, sky_w)
    row_share = local_coadd(gathered[0].astype(jnp.float32), gathered[1].astype(jnp.float32))
    copies = jnp.broadcast_to(row_share[None], (n_visit,) + row_share.shape)
    coadd_field = lax.all_to_all(copies, "visit", split_axis=0, concat_axis=0, tiled=True)
    bands = psf_bands(tap_rows)
    coadd_field = coadd_field.reshape(n_visit * chunk, sky_w)
    coadd_low = coadd_field.astype(jnp.bfloat16)

    all_starts = lax.all_gather(col_start[0], "sky", axis=0, tiled=True)
    windows = jnp.stack(
        [lax.dynamic_slice_in_dim(coadd_low, all_starts[peer], TILE, 1) for peer in range(n_sky)],
        axis=0,
    )
    strips_here = lax.all_to_all(windows, "sky", split_axis=0, concat_axis=0, tiled=True)
    footprint = jnp.concatenate(
        [lax.dynamic_index_in_dim(strips_here, strip_ids[slot], 0, keepdims=False) for slot in range(NOV)],
        axis=0,
    )
    projected = jnp.dot(row_interp[0, 0], footprint, preferred_element_type=jnp.float32).astype(
        jnp.bfloat16
    )
    blotted = jnp.dot(projected, col_interp[0, 0], preferred_element_type=jnp.float32).astype(
        jnp.bfloat16
    )
    matched = psf_match(blotted, bands)
    residual = (
        (science[0, 0].astype(jnp.float32) - matched)
        * inv_sigma[0, 0].astype(jnp.float32)
        / OUTLIER
    )
    outlier = 1.0 / (1.0 + residual * residual)
    return (coadd_field, outlier[None, None])


def solution(mesh):
    in_specs = (
        P("visit", "sky", None),
        P("visit", "sky", None),
        P("visit", "sky", None),
        P("visit", "sky"),
        P("visit", "sky", None, None),
        P("visit", "sky", None, None),
        P("visit", "sky", None, None),
        P("visit", "sky", None, None),
        P("visit", "sky", None, None),
        P("visit", "sky", None, None),
    )
    out_specs = (P("sky", None), P("visit", "sky", None, None))
    return jax.shard_map(shards, mesh=mesh, in_specs=in_specs, out_specs=out_specs, check_vma=False)
```

```python
import jax
import jax.numpy as jnp
from jax import lax
from jax.sharding import PartitionSpec as P


NOV = 4
TILE = 512
KSIZE = 11
CELL = 128
NCELL = 16
PASSES = 3


CAUCHY = 2.0
OUTLIER = 3.0


def local_coadd(values, weights):
    root_weight = jnp.sqrt(weights)
    coadd_field = jnp.sum(weights * values, axis=0) / jnp.sum(weights, axis=0)
    for _ in range(PASSES):
        scaled = (values - coadd_field[None]) * root_weight / CAUCHY
        cauchy = weights / (1.0 + scaled * scaled)
        coadd_field = jnp.sum(cauchy * values, axis=0) / jnp.sum(cauchy, axis=0)
    return coadd_field


def psf_taps(cell_grid, kernel_table):
    blocks = TILE // CELL
    picker = (cell_grid.reshape(-1)[:, None] == jnp.arange(NCELL, dtype=jnp.int32)[None, :]).astype(
        jnp.bfloat16
    )
    tap_rows = jnp.dot(picker, kernel_table, preferred_element_type=jnp.float32)
    return tap_rows.astype(jnp.bfloat16).reshape(blocks, blocks, KSIZE, KSIZE)


def psf_bands(tap_rows):
    blocks = TILE // CELL
    window = CELL + KSIZE - 1
    source = jnp.arange(window, dtype=jnp.int32)[:, None]
    target = jnp.arange(CELL, dtype=jnp.int32)[None, :]
    diagonal = (
        (source - target)[None] == jnp.arange(KSIZE, dtype=jnp.int32)[:, None, None]
    ).astype(jnp.bfloat16)
    banded_all = jnp.einsum(
        "xyab,bcl->xyacl", tap_rows, diagonal, preferred_element_type=jnp.float32
    ).astype(jnp.bfloat16)
    return tuple(banded_all[r, c] for r in range(blocks) for c in range(blocks))


def psf_match(blotted, bands):
    tile_side = blotted.shape[1]
    blocks = tile_side // CELL
    half_width = KSIZE // 2
    window = CELL + KSIZE - 1
    padded = jnp.pad(blotted, ((half_width, half_width), (half_width, half_width)))
    row_parts = []
    for row_block in range(blocks):
        rows_window = lax.slice_in_dim(padded, row_block * CELL, row_block * CELL + window, axis=0)
        col_parts = []
        for col_block in range(blocks):
            cols_window = lax.slice_in_dim(
                rows_window, col_block * CELL, col_block * CELL + window, axis=1
            )
            horizontal = jnp.einsum(
                "rc,acl->arl",
                cols_window,
                bands[row_block * blocks + col_block],
                preferred_element_type=jnp.float32,
            )
            summed = horizontal[0, 0:CELL, :]
            for tap_row in range(1, KSIZE):
                summed = summed + horizontal[tap_row, tap_row : tap_row + CELL, :]
            col_parts.append(summed)
        row_parts.append(jnp.concatenate(col_parts, axis=1))
    return jnp.concatenate(row_parts, axis=0)


def shards(
    warped,
    inv_var,
    intersection,
    col_start,
    row_interp,
    col_interp,
    cell_ids,
    kernels,
    science,
    inv_sigma,
):
    n_visit = lax.axis_size("visit")
    n_sky = lax.axis_size("sky")
    local_visits, strip_rows, sky_w = warped.shape
    stacked = jnp.stack([warped, inv_var], axis=0)
    tap_rows = psf_taps(cell_ids[0, 0], kernels[0, 0])
    stacked, tap_rows = lax.optimization_barrier((stacked, tap_rows))
    chunk = strip_rows // n_visit
    stacked = stacked.reshape(2, local_visits, n_visit, chunk, sky_w)
    gathered = lax.all_to_all(stacked, "visit", split_axis=2, concat_axis=1, tiled=True)
    gathered = gathered.reshape(2, local_visits * n_visit, chunk, sky_w)
    row_share = local_coadd(gathered[0].astype(jnp.float32), gathered[1].astype(jnp.float32))
    copies = jnp.broadcast_to(row_share[None], (n_visit,) + row_share.shape)
    coadd_field = lax.all_to_all(copies, "visit", split_axis=0, concat_axis=0, tiled=True)
    bands = psf_bands(tap_rows)
    coadd_field = coadd_field.reshape(n_visit * chunk, sky_w)
    coadd_low = coadd_field.astype(jnp.bfloat16)

    all_starts = lax.all_gather(col_start[0], "sky", axis=0, tiled=True)
    windows = jnp.stack(
        [lax.dynamic_slice_in_dim(coadd_low, all_starts[peer], TILE, 1) for peer in range(n_sky)],
        axis=0,
    )
    me = lax.axis_index("sky")
    received = [lax.dynamic_index_in_dim(windows, me, 0, keepdims=False)]
    for shift in range(1, n_sky):
        outgoing = lax.dynamic_index_in_dim(windows, (me + shift) % n_sky, 0, keepdims=False)
        received.append(
            lax.ppermute(
                outgoing, "sky", perm=[(i, (i + shift) % n_sky) for i in range(n_sky)]
            )
        )
    received = jnp.stack(received, axis=0)
    strips = intersection[0, 0]
    footprint = jnp.concatenate(
        [
            lax.dynamic_index_in_dim(received, (me - strips[slot]) % n_sky, 0, keepdims=False)
            for slot in range(NOV)
        ],
        axis=0,
    )
    projected = jnp.dot(row_interp[0, 0], footprint, preferred_element_type=jnp.float32).astype(
        jnp.bfloat16
    )
    blotted = jnp.dot(projected, col_interp[0, 0], preferred_element_type=jnp.float32).astype(
        jnp.bfloat16
    )
    matched = psf_match(blotted, bands)
    residual = (
        (science[0, 0].astype(jnp.float32) - matched)
        * inv_sigma[0, 0].astype(jnp.float32)
        / OUTLIER
    )
    outlier = 1.0 / (1.0 + residual * residual)
    return (coadd_field, outlier[None, None])


def solution(mesh):
    in_specs = (
        P("visit", "sky", None),
        P("visit", "sky", None),
        P("visit", "sky", None),
        P("visit", "sky"),
        P("visit", "sky", None, None),
        P("visit", "sky", None, None),
        P("visit", "sky", None, None),
        P("visit", "sky", None, None),
        P("visit", "sky", None, None),
        P("visit", "sky", None, None),
    )
    out_specs = (P("sky", None), P("visit", "sky", None, None))
    return jax.shard_map(shards, mesh=mesh, in_specs=in_specs, out_specs=out_specs, check_vma=False)
```

```python
import jax
import jax.numpy as jnp
from jax import lax
from jax.sharding import PartitionSpec as P


NOV = 4
TILE = 512
KSIZE = 11
CELL = 128
NCELL = 16
PASSES = 3


CAUCHY = 2.0
OUTLIER = 3.0


def local_coadd(values, weights):
    root_weight = jnp.sqrt(weights)
    coadd_field = jnp.sum(weights * values, axis=0) / jnp.sum(weights, axis=0)
    for _ in range(PASSES):
        scaled = (values - coadd_field[None]) * root_weight / CAUCHY
        cauchy = weights / (1.0 + scaled * scaled)
        coadd_field = jnp.sum(cauchy * values, axis=0) / jnp.sum(cauchy, axis=0)
    return coadd_field


def psf_taps(cell_grid, kernel_table):
    blocks = TILE // CELL
    picker = (cell_grid.reshape(-1)[:, None] == jnp.arange(NCELL, dtype=jnp.int32)[None, :]).astype(
        jnp.bfloat16
    )
    tap_rows = jnp.dot(picker, kernel_table, preferred_element_type=jnp.float32)
    return tap_rows.astype(jnp.bfloat16).reshape(blocks, blocks, KSIZE, KSIZE)


def psf_bands(tap_rows):
    blocks = TILE // CELL
    window = CELL + KSIZE - 1
    source = jnp.arange(window, dtype=jnp.int32)[:, None]
    target = jnp.arange(CELL, dtype=jnp.int32)[None, :]
    diagonal = (
        (source - target)[None] == jnp.arange(KSIZE, dtype=jnp.int32)[:, None, None]
    ).astype(jnp.bfloat16)
    banded_all = jnp.einsum(
        "xyab,bcl->xyacl", tap_rows, diagonal, preferred_element_type=jnp.float32
    ).astype(jnp.bfloat16)
    return tuple(banded_all[r, c] for r in range(blocks) for c in range(blocks))


def psf_match(blotted, bands):
    tile_side = blotted.shape[1]
    blocks = tile_side // CELL
    half_width = KSIZE // 2
    window = CELL + KSIZE - 1
    padded = jnp.pad(blotted, ((half_width, half_width), (half_width, half_width)))
    row_parts = []
    for row_block in range(blocks):
        rows_window = lax.slice_in_dim(padded, row_block * CELL, row_block * CELL + window, axis=0)
        col_parts = []
        for col_block in range(blocks):
            cols_window = lax.slice_in_dim(
                rows_window, col_block * CELL, col_block * CELL + window, axis=1
            )
            horizontal = jnp.einsum(
                "rc,acl->arl",
                cols_window,
                bands[row_block * blocks + col_block],
                preferred_element_type=jnp.float32,
            )
            summed = horizontal[0, 0:CELL, :]
            for tap_row in range(1, KSIZE):
                summed = summed + horizontal[tap_row, tap_row : tap_row + CELL, :]
            col_parts.append(summed)
        row_parts.append(jnp.concatenate(col_parts, axis=1))
    return jnp.concatenate(row_parts, axis=0)


def shards(
    warped,
    inv_var,
    intersection,
    col_start,
    row_interp,
    col_interp,
    cell_ids,
    kernels,
    science,
    inv_sigma,
):
    n_visit = lax.axis_size("visit")
    n_sky = lax.axis_size("sky")
    local_visits, strip_rows, sky_w = warped.shape
    stacked = jnp.stack([warped, inv_var], axis=0)
    tap_rows = psf_taps(cell_ids[0, 0], kernels[0, 0])
    stacked, tap_rows = lax.optimization_barrier((stacked, tap_rows))
    chunk = strip_rows // n_visit
    stacked = stacked.reshape(2, local_visits, n_visit, chunk, sky_w)
    gathered = lax.all_to_all(stacked, "visit", split_axis=2, concat_axis=1, tiled=True)
    gathered = gathered.reshape(2, local_visits * n_visit, chunk, sky_w)
    row_share = local_coadd(gathered[0].astype(jnp.float32), gathered[1].astype(jnp.float32))
    visit_me = lax.axis_index("visit")
    pieces = [row_share]
    for shift in range(1, n_visit):
        pieces.append(
            lax.ppermute(
                row_share, "visit", perm=[(i, (i + shift) % n_visit) for i in range(n_visit)]
            )
        )
    pieces = jnp.stack(pieces, axis=0)
    order = (visit_me - jnp.arange(n_visit, dtype=jnp.int32)) % n_visit
    coadd_field = jnp.take(pieces, order, axis=0)
    bands = psf_bands(tap_rows)
    coadd_field = coadd_field.reshape(n_visit * chunk, sky_w)
    coadd_low = coadd_field.astype(jnp.bfloat16)

    all_starts = lax.all_gather(col_start[0], "sky", axis=0, tiled=True)
    windows = jnp.stack(
        [lax.dynamic_slice_in_dim(coadd_low, all_starts[peer], TILE, 1) for peer in range(n_sky)],
        axis=0,
    )
    me = lax.axis_index("sky")
    received = [lax.dynamic_index_in_dim(windows, me, 0, keepdims=False)]
    for shift in range(1, n_sky):
        outgoing = lax.dynamic_index_in_dim(windows, (me + shift) % n_sky, 0, keepdims=False)
        received.append(
            lax.ppermute(
                outgoing, "sky", perm=[(i, (i + shift) % n_sky) for i in range(n_sky)]
            )
        )
    received = jnp.stack(received, axis=0)
    strips = intersection[0, 0]
    footprint = jnp.concatenate(
        [
            lax.dynamic_index_in_dim(received, (me - strips[slot]) % n_sky, 0, keepdims=False)
            for slot in range(NOV)
        ],
        axis=0,
    )
    projected = jnp.dot(row_interp[0, 0], footprint, preferred_element_type=jnp.float32).astype(
        jnp.bfloat16
    )
    blotted = jnp.dot(projected, col_interp[0, 0], preferred_element_type=jnp.float32).astype(
        jnp.bfloat16
    )
    matched = psf_match(blotted, bands)
    residual = (
        (science[0, 0].astype(jnp.float32) - matched)
        * inv_sigma[0, 0].astype(jnp.float32)
        / OUTLIER
    )
    outlier = 1.0 / (1.0 + residual * residual)
    return (coadd_field, outlier[None, None])


def solution(mesh):
    in_specs = (
        P("visit", "sky", None),
        P("visit", "sky", None),
        P("visit", "sky", None),
        P("visit", "sky"),
        P("visit", "sky", None, None),
        P("visit", "sky", None, None),
        P("visit", "sky", None, None),
        P("visit", "sky", None, None),
        P("visit", "sky", None, None),
        P("visit", "sky", None, None),
    )
    out_specs = (P("sky", None), P("visit", "sky", None, None))
    return jax.shard_map(shards, mesh=mesh, in_specs=in_specs, out_specs=out_specs, check_vma=False)
```

```python
import jax
import jax.numpy as jnp
from jax import lax
from jax.sharding import PartitionSpec as P


NOV = 4
TILE = 512
KSIZE = 11
CELL = 128
NCELL = 16
PASSES = 3


CAUCHY = 2.0
OUTLIER = 3.0


def local_coadd(values, weights):
    coadd_field = jnp.sum(weights * values, axis=0) / jnp.sum(weights, axis=0)
    square = CAUCHY * CAUCHY
    for _ in range(PASSES):
        offset = values - coadd_field[None]
        cauchy = (square * weights) / (square + offset * offset * weights)
        coadd_field = jnp.sum(cauchy * values, axis=0) / jnp.sum(cauchy, axis=0)
    return coadd_field


def psf_taps(cell_grid, kernel_table):
    blocks = TILE // CELL
    picker = (cell_grid.reshape(-1)[:, None] == jnp.arange(NCELL, dtype=jnp.int32)[None, :]).astype(
        jnp.bfloat16
    )
    tap_rows = jnp.dot(picker, kernel_table, preferred_element_type=jnp.float32)
    return tap_rows.astype(jnp.bfloat16).reshape(blocks, blocks, KSIZE, KSIZE)


def psf_bands(tap_rows):
    blocks = TILE // CELL
    window = CELL + KSIZE - 1
    source = jnp.arange(window, dtype=jnp.int32)[:, None]
    target = jnp.arange(CELL, dtype=jnp.int32)[None, :]
    diagonal = (
        (source - target)[None] == jnp.arange(KSIZE, dtype=jnp.int32)[:, None, None]
    ).astype(jnp.bfloat16)
    banded_all = jnp.einsum(
        "xyab,bcl->xyacl", tap_rows, diagonal, preferred_element_type=jnp.float32
    ).astype(jnp.bfloat16)
    return tuple(banded_all[r, c] for r in range(blocks) for c in range(blocks))


def psf_outlier(blotted, bands, science_tile, sigma_tile):
    tile_side = blotted.shape[1]
    blocks = tile_side // CELL
    half_width = KSIZE // 2
    window = CELL + KSIZE - 1
    padded = jnp.pad(blotted, ((half_width, half_width), (half_width, half_width)))
    row_parts = []
    for row_block in range(blocks):
        rows_window = lax.slice_in_dim(padded, row_block * CELL, row_block * CELL + window, axis=0)
        col_parts = []
        for col_block in range(blocks):
            cols_window = lax.slice_in_dim(
                rows_window, col_block * CELL, col_block * CELL + window, axis=1
            )
            horizontal = jnp.einsum(
                "rc,acl->arl",
                cols_window,
                bands[row_block * blocks + col_block],
                preferred_element_type=jnp.float32,
            )
            summed = horizontal[0, 0:CELL, :]
            for tap_row in range(1, KSIZE):
                summed = summed + horizontal[tap_row, tap_row : tap_row + CELL, :]
            rows = slice(row_block * CELL, (row_block + 1) * CELL)
            cols = slice(col_block * CELL, (col_block + 1) * CELL)
            residual = (
                (science_tile[rows, cols].astype(jnp.float32) - summed)
                * sigma_tile[rows, cols].astype(jnp.float32)
                / OUTLIER
            )
            col_parts.append(1.0 / (1.0 + residual * residual))
        row_parts.append(jnp.concatenate(col_parts, axis=1))
    return jnp.concatenate(row_parts, axis=0)


def shards(
    warped,
    inv_var,
    intersection,
    col_start,
    row_interp,
    col_interp,
    cell_ids,
    kernels,
    science,
    inv_sigma,
):
    n_visit = lax.axis_size("visit")
    n_sky = lax.axis_size("sky")
    local_visits, strip_rows, sky_w = warped.shape
    stacked = jnp.stack([warped, inv_var], axis=0)
    tap_rows = psf_taps(cell_ids[0, 0], kernels[0, 0])
    stacked, tap_rows = lax.optimization_barrier((stacked, tap_rows))
    chunk = strip_rows // n_visit
    stacked = stacked.reshape(2, local_visits, n_visit, chunk, sky_w)
    gathered = lax.all_to_all(stacked, "visit", split_axis=2, concat_axis=1, tiled=True)
    gathered = gathered.reshape(2, local_visits * n_visit, chunk, sky_w)
    row_share = local_coadd(gathered[0].astype(jnp.float32), gathered[1].astype(jnp.float32))
    copies = jnp.broadcast_to(row_share[None], (n_visit,) + row_share.shape)
    coadd_field = lax.all_to_all(copies, "visit", split_axis=0, concat_axis=0, tiled=True)
    bands = psf_bands(tap_rows)
    coadd_field = coadd_field.reshape(n_visit * chunk, sky_w)
    coadd_low = coadd_field.astype(jnp.bfloat16)

    all_starts = lax.all_gather(col_start[0], "sky", axis=0, tiled=True)
    windows = jnp.stack(
        [lax.dynamic_slice_in_dim(coadd_low, all_starts[peer], TILE, 1) for peer in range(n_sky)],
        axis=0,
    )
    me = lax.axis_index("sky")
    received = [lax.dynamic_index_in_dim(windows, me, 0, keepdims=False)]
    for shift in range(1, n_sky):
        outgoing = lax.dynamic_index_in_dim(windows, (me + shift) % n_sky, 0, keepdims=False)
        received.append(
            lax.ppermute(
                outgoing, "sky", perm=[(i, (i + shift) % n_sky) for i in range(n_sky)]
            )
        )
    received = jnp.stack(received, axis=0)
    strips = intersection[0, 0]
    footprint = jnp.concatenate(
        [
            lax.dynamic_index_in_dim(received, (me - strips[slot]) % n_sky, 0, keepdims=False)
            for slot in range(NOV)
        ],
        axis=0,
    )
    projected = jnp.dot(row_interp[0, 0], footprint, preferred_element_type=jnp.float32).astype(
        jnp.bfloat16
    )
    blotted = jnp.dot(projected, col_interp[0, 0], preferred_element_type=jnp.float32).astype(
        jnp.bfloat16
    )
    outlier = psf_outlier(blotted, bands, science[0, 0], inv_sigma[0, 0])
    return (coadd_field, outlier[None, None])


def solution(mesh):
    in_specs = (
        P("visit", "sky", None),
        P("visit", "sky", None),
        P("visit", "sky", None),
        P("visit", "sky"),
        P("visit", "sky", None, None),
        P("visit", "sky", None, None),
        P("visit", "sky", None, None),
        P("visit", "sky", None, None),
        P("visit", "sky", None, None),
        P("visit", "sky", None, None),
    )
    out_specs = (P("sky", None), P("visit", "sky", None, None))
    return jax.shard_map(shards, mesh=mesh, in_specs=in_specs, out_specs=out_specs, check_vma=False)
```

```python
import jax
import jax.numpy as jnp
from jax import lax
from jax.sharding import PartitionSpec as P


NOV = 4
TILE = 512
KSIZE = 11
CELL = 128
NCELL = 16
PASSES = 3


CAUCHY = 2.0
OUTLIER = 3.0


def local_coadd(values, weights):
    coadd_field = jnp.sum(weights * values, axis=0) / jnp.sum(weights, axis=0)
    square = CAUCHY * CAUCHY
    for _ in range(PASSES):
        offset = values - coadd_field[None]
        cauchy = (square * weights) / (square + offset * offset * weights)
        coadd_field = jnp.sum(cauchy * values, axis=0) / jnp.sum(cauchy, axis=0)
    return coadd_field


def psf_taps(cell_grid, kernel_table):
    blocks = TILE // CELL
    picker = (cell_grid.reshape(-1)[:, None] == jnp.arange(NCELL, dtype=jnp.int32)[None, :]).astype(
        jnp.bfloat16
    )
    tap_rows = jnp.dot(picker, kernel_table, preferred_element_type=jnp.float32)
    return tap_rows.astype(jnp.bfloat16).reshape(blocks, blocks, KSIZE, KSIZE)


def psf_bands(tap_rows):
    blocks = TILE // CELL
    window = CELL + KSIZE - 1
    source = jnp.arange(window, dtype=jnp.int32)[:, None]
    target = jnp.arange(CELL, dtype=jnp.int32)[None, :]
    diagonal = (
        (source - target)[None] == jnp.arange(KSIZE, dtype=jnp.int32)[:, None, None]
    ).astype(jnp.bfloat16)
    banded_all = jnp.einsum(
        "xyab,bcl->xyacl", tap_rows, diagonal, preferred_element_type=jnp.float32
    ).astype(jnp.bfloat16)
    return tuple(banded_all[r, c] for r in range(blocks) for c in range(blocks))


def psf_outlier(blotted, bands, science_tile, sigma_tile):
    tile_side = blotted.shape[1]
    blocks = tile_side // CELL
    half_width = KSIZE // 2
    window = CELL + KSIZE - 1
    padded = jnp.pad(blotted, ((half_width, half_width), (half_width, half_width)))
    outlier = jnp.zeros((tile_side, tile_side), jnp.float32)
    for row_block in range(blocks):
        rows_window = lax.slice_in_dim(padded, row_block * CELL, row_block * CELL + window, axis=0)
        for col_block in range(blocks):
            cols_window = lax.slice_in_dim(
                rows_window, col_block * CELL, col_block * CELL + window, axis=1
            )
            horizontal = jnp.einsum(
                "rc,acl->arl",
                cols_window,
                bands[row_block * blocks + col_block],
                preferred_element_type=jnp.float32,
            )
            summed = horizontal[0, 0:CELL, :]
            for tap_row in range(1, KSIZE):
                summed = summed + horizontal[tap_row, tap_row : tap_row + CELL, :]
            rows = slice(row_block * CELL, (row_block + 1) * CELL)
            cols = slice(col_block * CELL, (col_block + 1) * CELL)
            residual = (
                (science_tile[rows, cols].astype(jnp.float32) - summed)
                * sigma_tile[rows, cols].astype(jnp.float32)
                / OUTLIER
            )
            outlier = lax.dynamic_update_slice(
                outlier, 1.0 / (1.0 + residual * residual), (row_block * CELL, col_block * CELL)
            )
    return outlier


def shards(
    warped,
    inv_var,
    intersection,
    col_start,
    row_interp,
    col_interp,
    cell_ids,
    kernels,
    science,
    inv_sigma,
):
    n_visit = lax.axis_size("visit")
    n_sky = lax.axis_size("sky")
    local_visits, strip_rows, sky_w = warped.shape
    stacked = jnp.stack([warped, inv_var], axis=0)
    tap_rows = psf_taps(cell_ids[0, 0], kernels[0, 0])
    stacked, tap_rows = lax.optimization_barrier((stacked, tap_rows))
    chunk = strip_rows // n_visit
    stacked = stacked.reshape(2, local_visits, n_visit, chunk, sky_w)
    gathered = lax.all_to_all(stacked, "visit", split_axis=2, concat_axis=1, tiled=True)
    gathered = gathered.reshape(2, local_visits * n_visit, chunk, sky_w)
    row_share = local_coadd(gathered[0].astype(jnp.float32), gathered[1].astype(jnp.float32))
    copies = jnp.broadcast_to(row_share[None], (n_visit,) + row_share.shape)
    coadd_field = lax.all_to_all(copies, "visit", split_axis=0, concat_axis=0, tiled=True)
    bands = psf_bands(tap_rows)
    coadd_field = coadd_field.reshape(n_visit * chunk, sky_w)
    coadd_low = coadd_field.astype(jnp.bfloat16)

    all_starts = lax.all_gather(col_start[0], "sky", axis=0, tiled=True)
    windows = jnp.stack(
        [lax.dynamic_slice_in_dim(coadd_low, all_starts[peer], TILE, 1) for peer in range(n_sky)],
        axis=0,
    )
    me = lax.axis_index("sky")
    received = [lax.dynamic_index_in_dim(windows, me, 0, keepdims=False)]
    for shift in range(1, n_sky):
        outgoing = lax.dynamic_index_in_dim(windows, (me + shift) % n_sky, 0, keepdims=False)
        received.append(
            lax.ppermute(
                outgoing, "sky", perm=[(i, (i + shift) % n_sky) for i in range(n_sky)]
            )
        )
    strips = intersection[0, 0]
    slots = []
    for slot in range(NOV):
        shift_of = (me - strips[slot]) % n_sky
        chosen = received[0]
        for shift in range(1, n_sky):
            chosen = jnp.where(shift_of == shift, received[shift], chosen)
        slots.append(chosen)
    footprint = jnp.concatenate(slots, axis=0)
    projected = jnp.dot(row_interp[0, 0], footprint, preferred_element_type=jnp.float32).astype(
        jnp.bfloat16
    )
    blotted = jnp.dot(projected, col_interp[0, 0], preferred_element_type=jnp.float32).astype(
        jnp.bfloat16
    )
    outlier = psf_outlier(blotted, bands, science[0, 0], inv_sigma[0, 0])
    return (coadd_field, outlier[None, None])


def solution(mesh):
    in_specs = (
        P("visit", "sky", None),
        P("visit", "sky", None),
        P("visit", "sky", None),
        P("visit", "sky"),
        P("visit", "sky", None, None),
        P("visit", "sky", None, None),
        P("visit", "sky", None, None),
        P("visit", "sky", None, None),
        P("visit", "sky", None, None),
        P("visit", "sky", None, None),
    )
    out_specs = (P("sky", None), P("visit", "sky", None, None))
    return jax.shard_map(shards, mesh=mesh, in_specs=in_specs, out_specs=out_specs, check_vma=False)
```

```python
import jax
import jax.numpy as jnp
from jax import lax
from jax.sharding import PartitionSpec as P


NOV = 4
TILE = 512
KSIZE = 11
CELL = 128
NCELL = 16
PASSES = 3


CAUCHY = 2.0
OUTLIER = 3.0


def local_coadd(values, weights):
    coadd_field = jnp.sum(weights * values, axis=0) / jnp.sum(weights, axis=0)
    square = CAUCHY * CAUCHY
    for _ in range(PASSES):
        offset = values - coadd_field[None]
        cauchy = (square * weights) / (square + offset * offset * weights)
        coadd_field = jnp.sum(cauchy * values, axis=0) / jnp.sum(cauchy, axis=0)
    return coadd_field


def psf_taps(cell_grid, kernel_table):
    blocks = TILE // CELL
    picker = (cell_grid.reshape(-1)[:, None] == jnp.arange(NCELL, dtype=jnp.int32)[None, :]).astype(
        jnp.bfloat16
    )
    tap_rows = jnp.dot(picker, kernel_table, preferred_element_type=jnp.float32)
    return tap_rows.astype(jnp.bfloat16).reshape(blocks, blocks, KSIZE, KSIZE)


def psf_bands(tap_rows):
    blocks = TILE // CELL
    window = CELL + KSIZE - 1
    source = jnp.arange(window, dtype=jnp.int32)[:, None]
    target = jnp.arange(CELL, dtype=jnp.int32)[None, :]
    diagonal = (
        (source - target)[None] == jnp.arange(KSIZE, dtype=jnp.int32)[:, None, None]
    ).astype(jnp.bfloat16)
    banded_all = jnp.einsum(
        "xyab,bcl->xyacl", tap_rows, diagonal, preferred_element_type=jnp.float32
    ).astype(jnp.bfloat16)
    return tuple(banded_all[r, c] for r in range(blocks) for c in range(blocks))


def psf_outlier(blotted, bands, science_tile, sigma_tile):
    tile_side = blotted.shape[1]
    blocks = tile_side // CELL
    half_width = KSIZE // 2
    window = CELL + KSIZE - 1
    padded = jnp.pad(blotted, ((half_width, half_width), (half_width, half_width)))
    outlier = jnp.zeros((tile_side, tile_side), jnp.float32)
    for row_block in range(blocks):
        rows_window = lax.slice_in_dim(padded, row_block * CELL, row_block * CELL + window, axis=0)
        for col_block in range(blocks):
            cols_window = lax.slice_in_dim(
                rows_window, col_block * CELL, col_block * CELL + window, axis=1
            )
            horizontal = jnp.einsum(
                "rc,acl->arl",
                cols_window,
                bands[row_block * blocks + col_block],
                preferred_element_type=jnp.float32,
            )
            summed = horizontal[0, 0:CELL, :]
            for tap_row in range(1, KSIZE):
                summed = summed + horizontal[tap_row, tap_row : tap_row + CELL, :]
            rows = slice(row_block * CELL, (row_block + 1) * CELL)
            cols = slice(col_block * CELL, (col_block + 1) * CELL)
            residual = (
                (science_tile[rows, cols].astype(jnp.float32) - summed)
                * sigma_tile[rows, cols].astype(jnp.float32)
                / OUTLIER
            )
            outlier = lax.dynamic_update_slice(
                outlier, 1.0 / (1.0 + residual * residual), (row_block * CELL, col_block * CELL)
            )
    return outlier


def shards(
    warped,
    inv_var,
    intersection,
    col_start,
    row_interp,
    col_interp,
    cell_ids,
    kernels,
    science,
    inv_sigma,
):
    n_visit = lax.axis_size("visit")
    n_sky = lax.axis_size("sky")
    local_visits, strip_rows, sky_w = warped.shape
    stacked = jnp.stack([warped, inv_var], axis=0)
    tap_rows = psf_taps(cell_ids[0, 0], kernels[0, 0])
    stacked, tap_rows = lax.optimization_barrier((stacked, tap_rows))
    chunk = strip_rows // n_visit
    stacked = stacked.reshape(2, local_visits, n_visit, chunk, sky_w)
    gathered = lax.all_to_all(stacked, "visit", split_axis=2, concat_axis=1, tiled=True)
    gathered = gathered.reshape(2, local_visits * n_visit, chunk, sky_w)
    row_share = local_coadd(gathered[0].astype(jnp.float32), gathered[1].astype(jnp.float32))
    copies = jnp.broadcast_to(row_share[None], (n_visit,) + row_share.shape)
    coadd_field = lax.all_to_all(copies, "visit", split_axis=0, concat_axis=0, tiled=True)
    bands = psf_bands(tap_rows)
    coadd_field = coadd_field.reshape(n_visit * chunk, sky_w)
    coadd_low = coadd_field.astype(jnp.bfloat16)

    all_starts = lax.all_gather(col_start[0], "sky", axis=0, tiled=True)
    windows = jnp.stack(
        [lax.dynamic_slice_in_dim(coadd_low, all_starts[peer], TILE, 1) for peer in range(n_sky)],
        axis=0,
    )
    me = lax.axis_index("sky")
    received = [lax.dynamic_index_in_dim(windows, me, 0, keepdims=False)]
    for shift in range(1, n_sky):
        outgoing = lax.dynamic_index_in_dim(windows, (me + shift) % n_sky, 0, keepdims=False)
        received.append(
            lax.ppermute(
                outgoing, "sky", perm=[(i, (i + shift) % n_sky) for i in range(n_sky)]
            )
        )
    coadd_out = jnp.where(coadd_field == coadd_field, coadd_field, 0.0)
    received, coadd_out = lax.optimization_barrier((received, coadd_out))
    received = jnp.stack(received, axis=0)
    strips = intersection[0, 0]
    footprint = jnp.concatenate(
        [
            lax.dynamic_index_in_dim(received, (me - strips[slot]) % n_sky, 0, keepdims=False)
            for slot in range(NOV)
        ],
        axis=0,
    )
    projected = jnp.dot(row_interp[0, 0], footprint, preferred_element_type=jnp.float32).astype(
        jnp.bfloat16
    )
    blotted = jnp.dot(projected, col_interp[0, 0], preferred_element_type=jnp.float32).astype(
        jnp.bfloat16
    )
    outlier = psf_outlier(blotted, bands, science[0, 0], inv_sigma[0, 0])
    return (coadd_out, outlier[None, None])


def solution(mesh):
    in_specs = (
        P("visit", "sky", None),
        P("visit", "sky", None),
        P("visit", "sky", None),
        P("visit", "sky"),
        P("visit", "sky", None, None),
        P("visit", "sky", None, None),
        P("visit", "sky", None, None),
        P("visit", "sky", None, None),
        P("visit", "sky", None, None),
        P("visit", "sky", None, None),
    )
    out_specs = (P("sky", None), P("visit", "sky", None, None))
    return jax.shard_map(shards, mesh=mesh, in_specs=in_specs, out_specs=out_specs, check_vma=False)
```

```python
import jax
import jax.numpy as jnp
from jax import lax
from jax.sharding import PartitionSpec as P


NOV = 4
TILE = 512
KSIZE = 11
CELL = 128
PASSES = 3


CAUCHY = 2.0
OUTLIER = 3.0


def local_coadd(values, weights):
    coadd_field = jnp.sum(weights * values, axis=0) / jnp.sum(weights, axis=0)
    square = CAUCHY * CAUCHY
    for _ in range(PASSES):
        offset = values - coadd_field[None]
        cauchy = (square * weights) / (square + offset * offset * weights)
        coadd_field = jnp.sum(cauchy * values, axis=0) / jnp.sum(cauchy, axis=0)
    return coadd_field


def psf_taps(cell_grid, kernel_table):
    blocks = TILE // CELL
    tap_rows = jnp.take(kernel_table, cell_grid.reshape(-1), axis=0, mode="clip")
    return tap_rows.reshape(blocks, blocks, KSIZE, KSIZE)


def psf_bands(tap_rows):
    blocks = TILE // CELL
    window = CELL + KSIZE - 1
    source = jnp.arange(window, dtype=jnp.int32)[:, None]
    target = jnp.arange(CELL, dtype=jnp.int32)[None, :]
    diagonal = (
        (source - target)[None] == jnp.arange(KSIZE, dtype=jnp.int32)[:, None, None]
    ).astype(jnp.bfloat16)
    banded_all = jnp.einsum(
        "xyab,bcl->xyacl", tap_rows, diagonal, preferred_element_type=jnp.float32
    ).astype(jnp.bfloat16)
    return tuple(banded_all[r, c] for r in range(blocks) for c in range(blocks))


def psf_outlier(blotted, bands, science_tile, sigma_tile):
    tile_side = blotted.shape[1]
    blocks = tile_side // CELL
    half_width = KSIZE // 2
    window = CELL + KSIZE - 1
    padded = jnp.pad(blotted, ((half_width, half_width), (half_width, half_width)))
    outlier = jnp.zeros((tile_side, tile_side), jnp.float32)
    for row_block in range(blocks):
        rows_window = lax.slice_in_dim(padded, row_block * CELL, row_block * CELL + window, axis=0)
        for col_block in range(blocks):
            cols_window = lax.slice_in_dim(
                rows_window, col_block * CELL, col_block * CELL + window, axis=1
            )
            horizontal = jnp.einsum(
                "rc,acl->arl",
                cols_window,
                bands[row_block * blocks + col_block],
                preferred_element_type=jnp.float32,
            )
            summed = horizontal[0, 0:CELL, :]
            for tap_row in range(1, KSIZE):
                summed = summed + horizontal[tap_row, tap_row : tap_row + CELL, :]
            rows = slice(row_block * CELL, (row_block + 1) * CELL)
            cols = slice(col_block * CELL, (col_block + 1) * CELL)
            residual = (
                (science_tile[rows, cols].astype(jnp.float32) - summed)
                * sigma_tile[rows, cols].astype(jnp.float32)
                / OUTLIER
            )
            outlier = lax.dynamic_update_slice(
                outlier, 1.0 / (1.0 + residual * residual), (row_block * CELL, col_block * CELL)
            )
    return outlier


def shards(
    warped,
    inv_var,
    intersection,
    col_start,
    row_interp,
    col_interp,
    cell_ids,
    kernels,
    science,
    inv_sigma,
):
    n_visit = lax.axis_size("visit")
    n_sky = lax.axis_size("sky")
    local_visits, strip_rows, sky_w = warped.shape
    stacked = jnp.stack([warped, inv_var], axis=0)
    tap_rows = psf_taps(cell_ids[0, 0], kernels[0, 0])
    stacked, tap_rows = lax.optimization_barrier((stacked, tap_rows))
    chunk = strip_rows // n_visit
    stacked = stacked.reshape(2, local_visits, n_visit, chunk, sky_w)
    gathered = lax.all_to_all(stacked, "visit", split_axis=2, concat_axis=1, tiled=True)
    gathered = gathered.reshape(2, local_visits * n_visit, chunk, sky_w)
    row_share = local_coadd(gathered[0].astype(jnp.float32), gathered[1].astype(jnp.float32))
    copies = jnp.broadcast_to(row_share[None], (n_visit,) + row_share.shape)
    coadd_field = lax.all_to_all(copies, "visit", split_axis=0, concat_axis=0, tiled=True)
    bands = psf_bands(tap_rows)
    coadd_field = coadd_field.reshape(n_visit * chunk, sky_w)
    coadd_low = coadd_field.astype(jnp.bfloat16)

    all_starts = lax.all_gather(col_start[0], "sky", axis=0, tiled=True)
    windows = jnp.stack(
        [lax.dynamic_slice_in_dim(coadd_low, all_starts[peer], TILE, 1) for peer in range(n_sky)],
        axis=0,
    )
    me = lax.axis_index("sky")
    received = [lax.dynamic_index_in_dim(windows, me, 0, keepdims=False)]
    for shift in range(1, n_sky):
        outgoing = lax.dynamic_index_in_dim(windows, (me + shift) % n_sky, 0, keepdims=False)
        received.append(
            lax.ppermute(
                outgoing, "sky", perm=[(i, (i + shift) % n_sky) for i in range(n_sky)]
            )
        )
    coadd_out = jnp.where(coadd_field == coadd_field, coadd_field, 0.0)
    received, coadd_out = lax.optimization_barrier((received, coadd_out))
    received = jnp.stack(received, axis=0)
    strips = intersection[0, 0]
    footprint = jnp.concatenate(
        [
            lax.dynamic_index_in_dim(received, (me - strips[slot]) % n_sky, 0, keepdims=False)
            for slot in range(NOV)
        ],
        axis=0,
    )
    projected = jnp.dot(row_interp[0, 0], footprint, preferred_element_type=jnp.float32).astype(
        jnp.bfloat16
    )
    blotted = jnp.dot(projected, col_interp[0, 0], preferred_element_type=jnp.float32).astype(
        jnp.bfloat16
    )
    outlier = psf_outlier(blotted, bands, science[0, 0], inv_sigma[0, 0])
    return (coadd_out, outlier[None, None])


def solution(mesh):
    in_specs = (
        P("visit", "sky", None),
        P("visit", "sky", None),
        P("visit", "sky", None),
        P("visit", "sky"),
        P("visit", "sky", None, None),
        P("visit", "sky", None, None),
        P("visit", "sky", None, None),
        P("visit", "sky", None, None),
        P("visit", "sky", None, None),
        P("visit", "sky", None, None),
    )
    out_specs = (P("sky", None), P("visit", "sky", None, None))
    return jax.shard_map(shards, mesh=mesh, in_specs=in_specs, out_specs=out_specs, check_vma=False)
```

```python
import jax
import jax.numpy as jnp
from jax import lax
from jax.sharding import PartitionSpec as P


NOV = 4
TILE = 512
KSIZE = 11
CELL = 128
NCELL = 16
PASSES = 3


CAUCHY = 2.0
OUTLIER = 3.0


def local_coadd(values, weights):
    coadd_field = jnp.sum(weights * values, axis=0) / jnp.sum(weights, axis=0)
    square = CAUCHY * CAUCHY
    for _ in range(PASSES):
        offset = values - coadd_field[None]
        cauchy = (square * weights) / (square + offset * offset * weights)
        coadd_field = jnp.sum(cauchy * values, axis=0) / jnp.sum(cauchy, axis=0)
    return coadd_field


def psf_taps(cell_grid, kernel_table):
    blocks = TILE // CELL
    picker = (cell_grid.reshape(-1)[:, None] == jnp.arange(NCELL, dtype=jnp.int32)[None, :]).astype(
        jnp.bfloat16
    )
    tap_rows = jnp.dot(picker, kernel_table, preferred_element_type=jnp.float32)
    return tap_rows.astype(jnp.bfloat16).reshape(blocks, blocks, KSIZE, KSIZE)


def psf_bands(tap_rows):
    blocks = TILE // CELL
    window = CELL + KSIZE - 1
    source = jnp.arange(window, dtype=jnp.int32)[:, None]
    target = jnp.arange(CELL, dtype=jnp.int32)[None, :]
    diagonal = (
        (source - target)[None] == jnp.arange(KSIZE, dtype=jnp.int32)[:, None, None]
    ).astype(jnp.bfloat16)
    banded_all = jnp.einsum(
        "xyab,bcl->xyacl", tap_rows, diagonal, preferred_element_type=jnp.float32
    ).astype(jnp.bfloat16)
    return tuple(banded_all[r, c] for r in range(blocks) for c in range(blocks))


def psf_outlier(blotted, bands, science_tile, sigma_tile):
    tile_side = blotted.shape[1]
    blocks = tile_side // CELL
    half_width = KSIZE // 2
    window = CELL + KSIZE - 1
    padded = jnp.pad(blotted, ((half_width, half_width), (half_width, half_width)))
    outlier = jnp.zeros((tile_side, tile_side), jnp.float32)
    for row_block in range(blocks):
        rows_window = lax.slice_in_dim(padded, row_block * CELL, row_block * CELL + window, axis=0)
        for col_block in range(blocks):
            cols_window = lax.slice_in_dim(
                rows_window, col_block * CELL, col_block * CELL + window, axis=1
            )
            horizontal = jnp.einsum(
                "rc,acl->arl",
                cols_window,
                bands[row_block * blocks + col_block],
                preferred_element_type=jnp.float32,
            )
            summed = horizontal[0, 0:CELL, :]
            for tap_row in range(1, KSIZE):
                summed = summed + horizontal[tap_row, tap_row : tap_row + CELL, :]
            rows = slice(row_block * CELL, (row_block + 1) * CELL)
            cols = slice(col_block * CELL, (col_block + 1) * CELL)
            residual = (
                (science_tile[rows, cols].astype(jnp.float32) - summed)
                * sigma_tile[rows, cols].astype(jnp.float32)
                / OUTLIER
            )
            outlier = lax.dynamic_update_slice(
                outlier, 1.0 / (1.0 + residual * residual), (row_block * CELL, col_block * CELL)
            )
    return outlier


def shards(
    warped,
    inv_var,
    intersection,
    col_start,
    row_interp,
    col_interp,
    cell_ids,
    kernels,
    science,
    inv_sigma,
):
    n_visit = lax.axis_size("visit")
    n_sky = lax.axis_size("sky")
    local_visits, strip_rows, sky_w = warped.shape
    stacked = jnp.stack([warped, inv_var], axis=0)
    tap_rows = psf_taps(cell_ids[0, 0], kernels[0, 0])
    stacked, tap_rows = lax.optimization_barrier((stacked, tap_rows))
    chunk = strip_rows // n_visit
    stacked = stacked.reshape(2, local_visits, n_visit, chunk, sky_w)
    gathered = lax.all_to_all(stacked, "visit", split_axis=2, concat_axis=1, tiled=True)
    gathered = gathered.reshape(2, local_visits * n_visit, chunk, sky_w)
    row_share = local_coadd(gathered[0].astype(jnp.float32), gathered[1].astype(jnp.float32))
    copies = jnp.broadcast_to(row_share[None], (n_visit,) + row_share.shape)
    coadd_field = lax.all_to_all(copies, "visit", split_axis=0, concat_axis=0, tiled=True)
    bands = psf_bands(tap_rows)
    coadd_field = coadd_field.reshape(n_visit * chunk, sky_w)
    coadd_low = coadd_field.astype(jnp.bfloat16)

    me = lax.axis_index("sky")
    received = [lax.dynamic_slice_in_dim(coadd_low, col_start[0, 0], TILE, 1)]
    for shift in range(1, n_sky):
        peer_start = lax.ppermute(
            col_start[0], "sky", perm=[(i, (i - shift) % n_sky) for i in range(n_sky)]
        )
        outgoing = lax.dynamic_slice_in_dim(coadd_low, peer_start[0], TILE, 1)
        received.append(
            lax.ppermute(
                outgoing, "sky", perm=[(i, (i + shift) % n_sky) for i in range(n_sky)]
            )
        )
    coadd_out = jnp.where(coadd_field == coadd_field, coadd_field, 0.0)
    received, coadd_out = lax.optimization_barrier((received, coadd_out))
    received = jnp.stack(received, axis=0)
    strips = intersection[0, 0]
    footprint = jnp.concatenate(
        [
            lax.dynamic_index_in_dim(received, (me - strips[slot]) % n_sky, 0, keepdims=False)
            for slot in range(NOV)
        ],
        axis=0,
    )
    projected = jnp.dot(row_interp[0, 0], footprint, preferred_element_type=jnp.float32).astype(
        jnp.bfloat16
    )
    blotted = jnp.dot(projected, col_interp[0, 0], preferred_element_type=jnp.float32).astype(
        jnp.bfloat16
    )
    outlier = psf_outlier(blotted, bands, science[0, 0], inv_sigma[0, 0])
    return (coadd_out, outlier[None, None])


def solution(mesh):
    in_specs = (
        P("visit", "sky", None),
        P("visit", "sky", None),
        P("visit", "sky", None),
        P("visit", "sky"),
        P("visit", "sky", None, None),
        P("visit", "sky", None, None),
        P("visit", "sky", None, None),
        P("visit", "sky", None, None),
        P("visit", "sky", None, None),
        P("visit", "sky", None, None),
    )
    out_specs = (P("sky", None), P("visit", "sky", None, None))
    return jax.shard_map(shards, mesh=mesh, in_specs=in_specs, out_specs=out_specs, check_vma=False)
```

```python
import jax
import jax.numpy as jnp
from jax import lax
from jax.sharding import PartitionSpec as P


NOV = 4
TILE = 512
KSIZE = 11
CELL = 128
NCELL = 16
PASSES = 3


CAUCHY = 2.0
OUTLIER = 3.0


def local_coadd(values, weights):
    coadd_field = jnp.sum(weights * values, axis=0) / jnp.sum(weights, axis=0)
    square = CAUCHY * CAUCHY
    for _ in range(PASSES):
        offset = values - coadd_field[None]
        cauchy = (square * weights) / (square + offset * offset * weights)
        coadd_field = jnp.sum(cauchy * values, axis=0) / jnp.sum(cauchy, axis=0)
    return coadd_field


def psf_taps(cell_grid, kernel_table):
    blocks = TILE // CELL
    picker = (cell_grid.reshape(-1)[:, None] == jnp.arange(NCELL, dtype=jnp.int32)[None, :]).astype(
        jnp.bfloat16
    )
    tap_rows = jnp.dot(picker, kernel_table, preferred_element_type=jnp.float32)
    return tap_rows.astype(jnp.bfloat16).reshape(blocks, blocks, KSIZE, KSIZE)


def psf_bands(tap_rows):
    blocks = TILE // CELL
    window = CELL + KSIZE - 1
    source = jnp.arange(window, dtype=jnp.int32)[:, None]
    target = jnp.arange(CELL, dtype=jnp.int32)[None, :]
    diagonal = (
        (source - target)[None] == jnp.arange(KSIZE, dtype=jnp.int32)[:, None, None]
    ).astype(jnp.bfloat16)
    banded_all = jnp.einsum(
        "xyab,bcl->xyacl", tap_rows, diagonal, preferred_element_type=jnp.float32
    ).astype(jnp.bfloat16)
    return tuple(banded_all[r, c] for r in range(blocks) for c in range(blocks))


def psf_outlier(blotted, bands, science_tile, sigma_tile):
    tile_side = blotted.shape[1]
    blocks = tile_side // CELL
    half_width = KSIZE // 2
    window = CELL + KSIZE - 1
    padded = jnp.pad(blotted, ((half_width, half_width), (half_width, half_width)))
    outlier = jnp.zeros((tile_side, tile_side), jnp.float32)
    for row_block in range(blocks):
        rows_window = lax.slice_in_dim(padded, row_block * CELL, row_block * CELL + window, axis=0)
        for col_block in range(blocks):
            cols_window = lax.slice_in_dim(
                rows_window, col_block * CELL, col_block * CELL + window, axis=1
            )
            horizontal = jnp.einsum(
                "rc,acl->arl",
                cols_window,
                bands[row_block * blocks + col_block],
                preferred_element_type=jnp.float32,
            )
            summed = horizontal[0, 0:CELL, :]
            for tap_row in range(1, KSIZE):
                summed = summed + horizontal[tap_row, tap_row : tap_row + CELL, :]
            rows = slice(row_block * CELL, (row_block + 1) * CELL)
            cols = slice(col_block * CELL, (col_block + 1) * CELL)
            residual = (
                (science_tile[rows, cols].astype(jnp.float32) - summed)
                * sigma_tile[rows, cols].astype(jnp.float32)
                / OUTLIER
            )
            outlier = lax.dynamic_update_slice(
                outlier, 1.0 / (1.0 + residual * residual), (row_block * CELL, col_block * CELL)
            )
    return outlier


def shards(
    warped,
    inv_var,
    intersection,
    col_start,
    row_interp,
    col_interp,
    cell_ids,
    kernels,
    science,
    inv_sigma,
):
    n_visit = lax.axis_size("visit")
    n_sky = lax.axis_size("sky")
    local_visits, strip_rows, sky_w = warped.shape
    stacked = jnp.stack([warped, inv_var], axis=0)
    chunk = strip_rows // n_visit
    stacked = stacked.reshape(2, local_visits, n_visit, chunk, sky_w)
    gathered = lax.all_to_all(stacked, "visit", split_axis=2, concat_axis=1, tiled=True)
    gathered = gathered.reshape(2, local_visits * n_visit, chunk, sky_w)
    row_share = local_coadd(gathered[0].astype(jnp.float32), gathered[1].astype(jnp.float32))
    outer = n_visit // 2
    visit_me = lax.axis_index("visit")
    outer_me, inner_me = visit_me // 2, visit_me % 2
    same = [row_share]
    for shift in range(1, outer):
        same.append(
            lax.ppermute(
                row_share,
                "visit",
                perm=[(v, ((v // 2 + shift) % outer) * 2 + v % 2) for v in range(n_visit)],
            )
        )
    same = jnp.stack(same, axis=0)
    other = lax.ppermute(same, "visit", perm=[(v, v ^ 1) for v in range(n_visit)])
    both = jnp.stack([same, other], axis=0)
    pick_inner = jnp.arange(2, dtype=jnp.int32) ^ inner_me
    pick_outer = (outer_me - jnp.arange(outer, dtype=jnp.int32)) % outer
    coadd_field = jnp.take(jnp.take(both, pick_inner, axis=0), pick_outer, axis=1)
    coadd_field = coadd_field.transpose(1, 0, 2, 3)
    bands = psf_bands(psf_taps(cell_ids[0, 0], kernels[0, 0]))
    coadd_field = coadd_field.reshape(n_visit * chunk, sky_w)
    coadd_low = coadd_field.astype(jnp.bfloat16)

    me = lax.axis_index("sky")
    received = [lax.dynamic_slice_in_dim(coadd_low, col_start[0, 0], TILE, 1)]
    for shift in range(1, n_sky):
        peer_start = lax.ppermute(
            col_start[0], "sky", perm=[(i, (i - shift) % n_sky) for i in range(n_sky)]
        )
        outgoing = lax.dynamic_slice_in_dim(coadd_low, peer_start[0], TILE, 1)
        received.append(
            lax.ppermute(
                outgoing, "sky", perm=[(i, (i + shift) % n_sky) for i in range(n_sky)]
            )
        )
    coadd_out = jnp.where(coadd_field == coadd_field, coadd_field, 0.0)
    received, coadd_out = lax.optimization_barrier((received, coadd_out))
    received = jnp.stack(received, axis=0)
    strips = intersection[0, 0]
    footprint = jnp.concatenate(
        [
            lax.dynamic_index_in_dim(received, (me - strips[slot]) % n_sky, 0, keepdims=False)
            for slot in range(NOV)
        ],
        axis=0,
    )
    projected = jnp.dot(row_interp[0, 0], footprint, preferred_element_type=jnp.float32).astype(
        jnp.bfloat16
    )
    blotted = jnp.dot(projected, col_interp[0, 0], preferred_element_type=jnp.float32).astype(
        jnp.bfloat16
    )
    outlier = psf_outlier(blotted, bands, science[0, 0], inv_sigma[0, 0])
    return (coadd_out, outlier[None, None])


def solution(mesh):
    in_specs = (
        P("visit", "sky", None),
        P("visit", "sky", None),
        P("visit", "sky", None),
        P("visit", "sky"),
        P("visit", "sky", None, None),
        P("visit", "sky", None, None),
        P("visit", "sky", None, None),
        P("visit", "sky", None, None),
        P("visit", "sky", None, None),
        P("visit", "sky", None, None),
    )
    out_specs = (P("sky", None), P("visit", "sky", None, None))
    return jax.shard_map(shards, mesh=mesh, in_specs=in_specs, out_specs=out_specs, check_vma=False)
```

```python
import jax
import jax.numpy as jnp
from jax import lax
from jax.sharding import PartitionSpec as P


NOV = 4
TILE = 512
KSIZE = 11
CELL = 128
NCELL = 16
PASSES = 3


CAUCHY = 2.0
OUTLIER = 3.0


def local_coadd(values, weights):
    coadd_field = jnp.sum(weights * values, axis=0) / jnp.sum(weights, axis=0)
    square = CAUCHY * CAUCHY
    for _ in range(PASSES):
        offset = values - coadd_field[None]
        cauchy = (square * weights) / (square + offset * offset * weights)
        coadd_field = jnp.sum(cauchy * values, axis=0) / jnp.sum(cauchy, axis=0)
    return coadd_field


def psf_taps(cell_grid, kernel_table):
    blocks = TILE // CELL
    picker = (cell_grid.reshape(-1)[:, None] == jnp.arange(NCELL, dtype=jnp.int32)[None, :]).astype(
        jnp.bfloat16
    )
    tap_rows = jnp.dot(picker, kernel_table, preferred_element_type=jnp.float32)
    return tap_rows.astype(jnp.bfloat16).reshape(blocks, blocks, KSIZE, KSIZE)


def psf_bands(tap_rows):
    blocks = TILE // CELL
    window = CELL + KSIZE - 1
    source = jnp.arange(window, dtype=jnp.int32)[:, None]
    target = jnp.arange(CELL, dtype=jnp.int32)[None, :]
    diagonal = (
        (source - target)[None] == jnp.arange(KSIZE, dtype=jnp.int32)[:, None, None]
    ).astype(jnp.bfloat16)
    banded_all = jnp.einsum(
        "xyab,bcl->xyacl", tap_rows, diagonal, preferred_element_type=jnp.float32
    ).astype(jnp.bfloat16)
    return tuple(banded_all[r, c] for r in range(blocks) for c in range(blocks))


def psf_outlier(blotted, bands, science_tile, sigma_tile):
    tile_side = blotted.shape[1]
    blocks = tile_side // CELL
    half_width = KSIZE // 2
    window = CELL + KSIZE - 1
    padded = jnp.pad(blotted, ((half_width, half_width), (half_width, half_width)))
    outlier = jnp.zeros((tile_side, tile_side), jnp.float32)
    for row_block in range(blocks):
        rows_window = lax.slice_in_dim(padded, row_block * CELL, row_block * CELL + window, axis=0)
        for col_block in range(blocks):
            cols_window = lax.slice_in_dim(
                rows_window, col_block * CELL, col_block * CELL + window, axis=1
            )
            horizontal = jnp.einsum(
                "rc,acl->arl",
                cols_window,
                bands[row_block * blocks + col_block],
                preferred_element_type=jnp.float32,
            )
            summed = horizontal[0, 0:CELL, :]
            for tap_row in range(1, KSIZE):
                summed = summed + horizontal[tap_row, tap_row : tap_row + CELL, :]
            rows = slice(row_block * CELL, (row_block + 1) * CELL)
            cols = slice(col_block * CELL, (col_block + 1) * CELL)
            residual = (
                (science_tile[rows, cols].astype(jnp.float32) - summed)
                * sigma_tile[rows, cols].astype(jnp.float32)
                / OUTLIER
            )
            outlier = lax.dynamic_update_slice(
                outlier, 1.0 / (1.0 + residual * residual), (row_block * CELL, col_block * CELL)
            )
    return outlier


def shards(
    warped,
    inv_var,
    intersection,
    col_start,
    row_interp,
    col_interp,
    cell_ids,
    kernels,
    science,
    inv_sigma,
):
    n_visit = lax.axis_size("visit")
    n_sky = lax.axis_size("sky")
    local_visits, strip_rows, sky_w = warped.shape
    stacked = jnp.stack([warped, inv_var], axis=0)
    chunk = strip_rows // n_visit
    stacked = stacked.reshape(2, local_visits, n_visit, chunk, sky_w)
    gathered = lax.all_to_all(stacked, "visit", split_axis=2, concat_axis=1, tiled=True)
    gathered = gathered.reshape(2, local_visits * n_visit, chunk, sky_w)
    row_share = local_coadd(gathered[0].astype(jnp.float32), gathered[1].astype(jnp.float32))
    outer = n_visit // 2
    visit_me = lax.axis_index("visit")
    outer_me, inner_me = visit_me // 2, visit_me % 2
    pick_inner = jnp.arange(2, dtype=jnp.int32) ^ inner_me
    pick_outer = (outer_me - jnp.arange(outer, dtype=jnp.int32)) % outer

    def outer_stage(part):
        same = [part]
        for shift in range(1, outer):
            same.append(
                lax.ppermute(
                    part,
                    "visit",
                    perm=[(v, ((v // 2 + shift) % outer) * 2 + v % 2) for v in range(n_visit)],
                )
            )
        return jnp.stack(same, axis=0)

    def inner_stage(same):
        other = lax.ppermute(same, "visit", perm=[(v, v ^ 1) for v in range(n_visit)])
        both = jnp.stack([same, other], axis=0)
        return jnp.take(jnp.take(both, pick_inner, axis=0), pick_outer, axis=1)

    half = chunk // 2
    same_first = outer_stage(row_share[:half])
    second, same_first = lax.optimization_barrier((row_share[half:], same_first))
    same_second = outer_stage(second)
    coadd_field = jnp.concatenate(
        [inner_stage(same_first), inner_stage(same_second)], axis=2
    )
    coadd_field = coadd_field.transpose(1, 0, 2, 3)
    bands = psf_bands(psf_taps(cell_ids[0, 0], kernels[0, 0]))
    coadd_field = coadd_field.reshape(n_visit * chunk, sky_w)
    coadd_low = coadd_field.astype(jnp.bfloat16)

    me = lax.axis_index("sky")
    received = [lax.dynamic_slice_in_dim(coadd_low, col_start[0, 0], TILE, 1)]
    for shift in range(1, n_sky):
        peer_start = lax.ppermute(
            col_start[0], "sky", perm=[(i, (i - shift) % n_sky) for i in range(n_sky)]
        )
        outgoing = lax.dynamic_slice_in_dim(coadd_low, peer_start[0], TILE, 1)
        received.append(
            lax.ppermute(
                outgoing, "sky", perm=[(i, (i + shift) % n_sky) for i in range(n_sky)]
            )
        )
    coadd_out = jnp.where(coadd_field == coadd_field, coadd_field, 0.0)
    received, coadd_out = lax.optimization_barrier((received, coadd_out))
    received = jnp.stack(received, axis=0)
    strips = intersection[0, 0]
    footprint = jnp.concatenate(
        [
            lax.dynamic_index_in_dim(received, (me - strips[slot]) % n_sky, 0, keepdims=False)
            for slot in range(NOV)
        ],
        axis=0,
    )
    projected = jnp.dot(row_interp[0, 0], footprint, preferred_element_type=jnp.float32).astype(
        jnp.bfloat16
    )
    blotted = jnp.dot(projected, col_interp[0, 0], preferred_element_type=jnp.float32).astype(
        jnp.bfloat16
    )
    outlier = psf_outlier(blotted, bands, science[0, 0], inv_sigma[0, 0])
    return (coadd_out, outlier[None, None])


def solution(mesh):
    in_specs = (
        P("visit", "sky", None),
        P("visit", "sky", None),
        P("visit", "sky", None),
        P("visit", "sky"),
        P("visit", "sky", None, None),
        P("visit", "sky", None, None),
        P("visit", "sky", None, None),
        P("visit", "sky", None, None),
        P("visit", "sky", None, None),
        P("visit", "sky", None, None),
    )
    out_specs = (P("sky", None), P("visit", "sky", None, None))
    return jax.shard_map(shards, mesh=mesh, in_specs=in_specs, out_specs=out_specs, check_vma=False)
```

```python
import jax
import jax.numpy as jnp
from jax import lax
from jax.sharding import PartitionSpec as P


NOV = 4
TILE = 512
KSIZE = 11
CELL = 128
NCELL = 16
PASSES = 3


CAUCHY = 2.0
OUTLIER = 3.0


def local_coadd(values, weights):
    coadd_field = jnp.sum(weights * values, axis=0) / jnp.sum(weights, axis=0)
    square = CAUCHY * CAUCHY
    for _ in range(PASSES):
        offset = values - coadd_field[None]
        cauchy = (square * weights) / (square + offset * offset * weights)
        coadd_field = jnp.sum(cauchy * values, axis=0) / jnp.sum(cauchy, axis=0)
    return coadd_field


def psf_taps(cell_grid, kernel_table):
    blocks = TILE // CELL
    picker = (cell_grid.reshape(-1)[:, None] == jnp.arange(NCELL, dtype=jnp.int32)[None, :]).astype(
        jnp.bfloat16
    )
    tap_rows = jnp.dot(picker, kernel_table, preferred_element_type=jnp.float32)
    return tap_rows.astype(jnp.bfloat16).reshape(blocks, blocks, KSIZE, KSIZE)


def psf_bands(tap_rows):
    blocks = TILE // CELL
    window = CELL + KSIZE - 1
    source = jnp.arange(window, dtype=jnp.int32)[:, None]
    target = jnp.arange(CELL, dtype=jnp.int32)[None, :]
    diagonal = (
        (source - target)[None] == jnp.arange(KSIZE, dtype=jnp.int32)[:, None, None]
    ).astype(jnp.bfloat16)
    banded_all = jnp.einsum(
        "xyab,bcl->xyacl", tap_rows, diagonal, preferred_element_type=jnp.float32
    ).astype(jnp.bfloat16)
    return tuple(banded_all[r, c] for r in range(blocks) for c in range(blocks))


def psf_outlier(blotted, bands, science_tile, sigma_tile):
    tile_side = blotted.shape[1]
    blocks = tile_side // CELL
    half_width = KSIZE // 2
    window = CELL + KSIZE - 1
    padded = jnp.pad(blotted, ((half_width, half_width), (half_width, half_width)))
    padded = lax.optimization_barrier(padded)
    outlier = jnp.zeros((tile_side, tile_side), jnp.float32)
    for row_block in range(blocks):
        rows_window = lax.slice_in_dim(padded, row_block * CELL, row_block * CELL + window, axis=0)
        for col_block in range(blocks):
            cols_window = lax.slice_in_dim(
                rows_window, col_block * CELL, col_block * CELL + window, axis=1
            )
            horizontal = jnp.einsum(
                "rc,acl->arl",
                cols_window,
                bands[row_block * blocks + col_block],
                preferred_element_type=jnp.float32,
            )
            summed = horizontal[0, 0:CELL, :]
            for tap_row in range(1, KSIZE):
                summed = summed + horizontal[tap_row, tap_row : tap_row + CELL, :]
            rows = slice(row_block * CELL, (row_block + 1) * CELL)
            cols = slice(col_block * CELL, (col_block + 1) * CELL)
            residual = (
                (science_tile[rows, cols].astype(jnp.float32) - summed)
                * sigma_tile[rows, cols].astype(jnp.float32)
                / OUTLIER
            )
            outlier = lax.dynamic_update_slice(
                outlier, 1.0 / (1.0 + residual * residual), (row_block * CELL, col_block * CELL)
            )
    return outlier


def shards(
    warped,
    inv_var,
    intersection,
    col_start,
    row_interp,
    col_interp,
    cell_ids,
    kernels,
    science,
    inv_sigma,
):
    n_visit = lax.axis_size("visit")
    n_sky = lax.axis_size("sky")
    local_visits, strip_rows, sky_w = warped.shape
    stacked = jnp.stack([warped, inv_var], axis=0)
    chunk = strip_rows // n_visit
    stacked = stacked.reshape(2, local_visits, n_visit, chunk, sky_w)
    gathered = lax.all_to_all(stacked, "visit", split_axis=2, concat_axis=1, tiled=True)
    gathered = gathered.reshape(2, local_visits * n_visit, chunk, sky_w)
    row_share = local_coadd(gathered[0].astype(jnp.float32), gathered[1].astype(jnp.float32))
    copies = jnp.broadcast_to(row_share[None], (n_visit,) + row_share.shape)
    coadd_field = lax.all_to_all(copies, "visit", split_axis=0, concat_axis=0, tiled=True)
    bands = psf_bands(psf_taps(cell_ids[0, 0], kernels[0, 0]))
    coadd_field = coadd_field.reshape(n_visit * chunk, sky_w)
    coadd_low = coadd_field.astype(jnp.bfloat16)

    me = lax.axis_index("sky")
    received = [lax.dynamic_slice_in_dim(coadd_low, col_start[0, 0], TILE, 1)]
    for shift in range(1, n_sky):
        peer_start = lax.ppermute(
            col_start[0], "sky", perm=[(i, (i - shift) % n_sky) for i in range(n_sky)]
        )
        outgoing = lax.dynamic_slice_in_dim(coadd_low, peer_start[0], TILE, 1)
        received.append(
            lax.ppermute(
                outgoing, "sky", perm=[(i, (i + shift) % n_sky) for i in range(n_sky)]
            )
        )
    coadd_out = jnp.where(coadd_field == coadd_field, coadd_field, 0.0)
    received, coadd_out = lax.optimization_barrier((received, coadd_out))
    received = jnp.stack(received, axis=0)
    strips = intersection[0, 0]
    footprint = jnp.concatenate(
        [
            lax.dynamic_index_in_dim(received, (me - strips[slot]) % n_sky, 0, keepdims=False)
            for slot in range(NOV)
        ],
        axis=0,
    )
    projected = jnp.dot(row_interp[0, 0], footprint, preferred_element_type=jnp.float32).astype(
        jnp.bfloat16
    )
    projected = lax.optimization_barrier(projected)
    blotted = jnp.dot(projected, col_interp[0, 0], preferred_element_type=jnp.float32).astype(
        jnp.bfloat16
    )
    outlier = psf_outlier(blotted, bands, science[0, 0], inv_sigma[0, 0])
    return (coadd_out, outlier[None, None])


def solution(mesh):
    in_specs = (
        P("visit", "sky", None),
        P("visit", "sky", None),
        P("visit", "sky", None),
        P("visit", "sky"),
        P("visit", "sky", None, None),
        P("visit", "sky", None, None),
        P("visit", "sky", None, None),
        P("visit", "sky", None, None),
        P("visit", "sky", None, None),
        P("visit", "sky", None, None),
    )
    out_specs = (P("sky", None), P("visit", "sky", None, None))
    return jax.shard_map(shards, mesh=mesh, in_specs=in_specs, out_specs=out_specs, check_vma=False)
```
